32 devices in a mesh: rep: 4 (over y, x), shard: 8 (over z, core).
Axes of the slice: x: 2, y: 2, z: 4, core: 2. Of those that a mesh axis runs over, the one named last changes fastest.
Arguments:
- activations: bfloat16 [49152, 1280], P(('rep', 'shard')), may hold values from -6 to 6
- cotangents: bfloat16 [49152, 1280], P(('rep', 'shard')), may hold values from -6 to 6
- grad_vectors: bfloat16 [32, 2, 1280], P(('rep', 'shard')), may hold values from -448 to 448
- master_matrix: float32 [1280, 1280], P('shard'), may hold values from -600 to 600
- first_matrix: float32 [1280, 1280], P('shard'), may hold values from -800 to 800
- second_matrix: float32 [1280, 1280], P('shard'), may hold values from 0.3 to 3.2
- master_vector: float32 [2, 1280], P(None, 'shard'), may hold values from 0.05 to 1
- first_vector: float32 [2, 1280], P(None, 'shard'), may hold values from -4 to 4
- second_vector: float32 [2, 1280], P(None, 'shard'), may hold values from 0.1 to 1
Outputs:
- gathered_matrix: bfloat16 [1280, 1280], replicated
- gathered_vectors: bfloat16 [2, 1280], replicated
- master_rows: float32 [1280, 1280], P('shard')
- first_rows: float32 [1280, 1280], P('shard')
- second_rows: float32 [1280, 1280], P('shard')
- master_vectors: float32 [2, 1280], P(None, 'shard')
- first_vectors: float32 [2, 1280], P(None, 'shard')
- second_vectors: float32 [2, 1280], P(None, 'shard')
The draws below stay inside these ranges and needn't reach their ends.
All inputs are finite; a program needn't handle non-finite values.
Results may differ from the reference program's by a relative error of at most 0.0004.
Values may be sent and summed in bfloat16 or wider, within the bound.
No kernel may reach another device: no remote copies, remote signals or barrier semaphores. Data moves between devices by JAX's collectives and lax.ppermute only.
A program may use at most 64 MiB of HBM per device.

```python
import math
import jax
import jax.numpy as jnp
from jax import lax

D = 1280
TOK_DEV = 1536
ALL_TOKENS = 49152
DEVICES = 32


def scale_table(key):
    folded = jax.random.fold_in(key, 21)
    key_row, key_col = jax.random.split(folded)
    rise = jnp.arange(D, dtype=jnp.float32)[:, None] / D * 3.0 - 1.5
    row_scale = 10.0 ** (rise + jax.random.uniform(key_row, (D, 1), jnp.float32, 0.0, 0.3))
    col_scale = 10.0 ** jax.random.uniform(key_col, (1, D), jnp.float32, 0.0, 0.3)
    return row_scale * col_scale


def draw_master_matrix(key, part):
    folded = jax.random.fold_in(key, 11)
    table = scale_table(key)
    base = jax.random.truncated_normal(folded, -4.0, 4.0, (D, D), jnp.float32)
    return base * table


def draw_first_matrix(key, part):
    folded = jax.random.fold_in(key, 12)
    table = scale_table(key)
    base = jax.random.truncated_normal(folded, -4.0, 4.0, (D, D), jnp.float32)
    return base * table * 1.5


def draw_second_matrix(key, part):
    folded = jax.random.fold_in(key, 13)
    return 10.0 ** jax.random.uniform(folded, (D, D), jnp.float32, -0.5, 0.5)


def strengthened(array, key, source, target, blocks, factor):
    def block_of(dim):
        return (jnp.arange(array.shape[dim]) // (array.shape[dim] // blocks)).reshape((-1,) + (1,) * (array.ndim - 1 - dim))

    one_side = jax.random.permutation(key, blocks)[block_of(target)]
    other_side = (block_of(target) + blocks // 2) % blocks
    return jnp.where((block_of(source) == one_side) | (block_of(source) == other_side), factor * array, array)


def block_scale(rng, dims, shards, smallest, top_value):
    level, own = 1.0, jax.random.fold_in(rng, 6)
    for position, blocks in shards:
        steps = jnp.exp(jax.random.uniform(jax.random.fold_in(own, position), (blocks,), jnp.float32, smallest / len(shards), top_value / len(shards)))
        level = level * jnp.repeat(steps, dims[position] // blocks).reshape([-1 if axis == position else 1 for axis in range(len(dims))])
    return level


def centred(rng, shape, width, reach, pieces=(), kind=jnp.bfloat16):
    gain = block_scale(rng, shape, pieces, -0.22, 0.18) if pieces else 1.0
    drawn = jax.random.normal(rng, shape, jnp.float32) * width * gain
    return jnp.minimum(jnp.maximum(drawn, -reach), reach).astype(kind)


def heavy_noise(key, extent, spread, bound, pieces, heavy, kind=jnp.bfloat16):
    values = spread * jax.random.normal(key, extent, jnp.float32)
    if pieces:
        values = values * block_scale(key, extent, pieces, -0.22, 0.18)
    return jnp.clip(strengthened(values, jax.random.fold_in(key, 3), *heavy), -bound, bound).astype(kind)


def setup_inputs(seed: int = 0) -> dict:
    streams_of = jax.random.split(jax.random.key(seed), 10)
    return {
        "activations": centred(streams_of[0], (ALL_TOKENS, D), 1.0, 6.0, ((0, 32),)),
        "cotangents": heavy_noise(streams_of[1], (ALL_TOKENS, D), 1.0, 6.0, ((0, 32),), (0, 1, 32, 2.75)),
        "grad_vectors": heavy_noise(streams_of[2], (DEVICES, 2, D), (TOK_DEV ** 0.5), 448.0, ((0, 32),), (0, 2, 32, 2.75)),
        "master_matrix": draw_master_matrix(jax.random.fold_in(streams_of[9], 71), 0),
        "first_matrix": draw_first_matrix(jax.random.fold_in(streams_of[9], 71), 0),
        "second_matrix": draw_second_matrix(jax.random.fold_in(streams_of[9], 71), 0),
        "master_vector": jnp.clip(jnp.exp(math.log(1.0) - 2.9957323 * jax.random.uniform(streams_of[6], (2, D), jnp.float32) ** block_scale(streams_of[6], (2, D), ((1, 8),), -0.2, 0.2)), 0.05, 1.0),
        "first_vector": centred(streams_of[7], (2, D), 0.3, 4.0, ((1, 8),), jnp.float32),
        "second_vector": jnp.clip(jnp.exp(math.log(1.0) - 2.3025851 * jax.random.uniform(streams_of[8], (2, D), jnp.float32) ** block_scale(streams_of[8], (2, D), ((1, 8),), -0.2, 0.2)), 0.1, 1.0),
    }


beta_one = 0.9
beta_two = 0.95
adam_eps = 1e-08
decay_rate = 0.1
learn_rate = 0.2
bias_one = 0.9999734386011124
bias_two = 0.994079470779666
norm_eps = 1e-06

def moments(gradient, moment_one, moment_two):
    fresh_one = beta_one * moment_one + (1.0 - beta_one) * gradient
    fresh_two = beta_two * moment_two + (1.0 - beta_two) * gradient * gradient
    return (fresh_one, fresh_two)

def direction_of(fresh_one, fresh_two, master):
    return fresh_one / bias_one / (jnp.sqrt(fresh_two / bias_two) + adam_eps) + decay_rate * master

def reference(activations, cotangents, grad_vectors, master_matrix, first_matrix, second_matrix, master_vector, first_vector, second_vector):
    grad_scale = 1.0 / math.sqrt(ALL_TOKENS)
    grad_matrix = lax.dot_general(cotangents, activations, (((0,), (0,)), ((), ())), preferred_element_type=jnp.float32) * grad_scale
    grad_vec = lax.optimization_barrier(jnp.sum(grad_vectors.astype(jnp.float32), axis=0)) * grad_scale
    first_rows, second_rows = moments(grad_matrix, first_matrix, second_matrix)
    first_vecs, second_vecs = moments(grad_vec, first_vector, second_vector)
    update_matrix = direction_of(first_rows, second_rows, master_matrix)
    update_vec = direction_of(first_vecs, second_vecs, master_vector)
    trust_matrix = jnp.sqrt(jnp.sum(master_matrix * master_matrix)) / jnp.sqrt(jnp.sum(update_matrix * update_matrix) + norm_eps)
    trust_vec = jnp.sqrt(lax.optimization_barrier(jnp.sum(master_vector * master_vector, axis=1, keepdims=True))) / jnp.sqrt(lax.optimization_barrier(jnp.sum(update_vec * update_vec, axis=1, keepdims=True)) + norm_eps)
    stepped = master_matrix - learn_rate * trust_matrix * update_matrix
    master_rows = stepped / jnp.sqrt(lax.optimization_barrier(jnp.mean(stepped * stepped, axis=1, keepdims=True)) + norm_eps)
    master_vecs = master_vector - learn_rate * trust_vec * update_vec
    return (master_rows.astype(jnp.bfloat16), master_vecs.astype(jnp.bfloat16), master_rows, first_rows, second_rows, master_vecs, first_vecs, second_vecs)
```

```python
import math

import jax
import jax.numpy as jnp
from jax import lax
from jax.sharding import PartitionSpec as P

beta_one = 0.9
beta_two = 0.95
adam_eps = 1e-08
decay_rate = 0.1
learn_rate = 0.2
bias_one = 0.9999734386011124
bias_two = 0.994079470779666
norm_eps = 1e-06


def moments(gradient, moment_one, moment_two):
    fresh_one = beta_one * moment_one + (1.0 - beta_one) * gradient
    fresh_two = beta_two * moment_two + (1.0 - beta_two) * gradient * gradient
    return (fresh_one, fresh_two)


def direction_of(fresh_one, fresh_two, master):
    return fresh_one / bias_one / (jnp.sqrt(fresh_two / bias_two) + adam_eps) + decay_rate * master


def per_device(
    activations,
    cotangents,
    grad_vectors,
    master_matrix,
    first_matrix,
    second_matrix,
    master_vector,
    first_vector,
    second_vector,
):
    rep_count = lax.axis_size("rep")
    shard_count = lax.axis_size("shard")
    tok_count, model_width = activations.shape
    rows = master_matrix.shape[0]
    grad_scale = 1.0 / math.sqrt(tok_count * rep_count * shard_count)
    weight_sq = jnp.sum(master_matrix * master_matrix)
    vector_sq = jnp.sum(master_vector * master_vector, axis=1)
    contract = (((0,), (0,)), ((), ()))
    grad_term = (
        lax.dot_general(cotangents, activations, contract, preferred_element_type=jnp.float32)
        * grad_scale
    )
    vector_term = grad_vectors[0].astype(jnp.float32) * grad_scale
    vector_rows = vector_term.reshape(2, shard_count, rows).transpose(1, 0, 2)
    vector_rows = vector_rows.reshape(shard_count, 1, 2 * rows)
    vector_rows = jnp.pad(vector_rows, ((0, 0), (0, 7), (0, model_width - 2 * rows)))
    blocks = jnp.concatenate(
        [grad_term.reshape(shard_count, rows, model_width), vector_rows], axis=1
    ).reshape(shard_count * (rows + 8), model_width)
    shard_grad = lax.psum_scatter(blocks, "shard", scatter_dimension=0, tiled=True)
    summed = lax.psum(shard_grad, "rep")
    grad_rows = summed[:rows]
    grad_vecs = summed[rows, : 2 * rows].reshape(2, rows)
    first_rows, second_rows = moments(grad_rows, first_matrix, second_matrix)
    first_vecs, second_vecs = moments(grad_vecs, first_vector, second_vector)
    update_matrix = direction_of(first_rows, second_rows, master_matrix)
    update_vec = direction_of(first_vecs, second_vecs, master_vector)
    update_sq = jnp.sum(update_matrix * update_matrix)
    upvector_sq = jnp.sum(update_vec * update_vec, axis=1)
    weight_tot, vector_tot, update_tot, upvector_tot = lax.psum(
        (weight_sq, vector_sq, update_sq, upvector_sq), "shard"
    )
    trust_matrix = jnp.sqrt(weight_tot) / jnp.sqrt(update_tot + norm_eps)
    trust_vec = (jnp.sqrt(vector_tot) / jnp.sqrt(upvector_tot + norm_eps))[:, None]
    stepped = master_matrix - learn_rate * trust_matrix * update_matrix
    master_rows = stepped / jnp.sqrt(jnp.mean(stepped * stepped, axis=1, keepdims=True) + norm_eps)
    master_vecs = master_vector - learn_rate * trust_vec * update_vec
    vec_row = master_vecs.astype(jnp.bfloat16).reshape(1, 2 * rows)
    vec_row = jnp.pad(vec_row, ((0, 15), (0, model_width - 2 * rows)))
    send = jnp.concatenate([master_rows.astype(jnp.bfloat16), vec_row], axis=0)
    gathered = lax.all_gather(send, "shard", axis=0, tiled=True)
    gathered = gathered.reshape(shard_count, rows + 16, model_width)
    gathered_matrix = gathered[:, :rows].reshape(shard_count * rows, model_width)
    gathered_vectors = gathered[:, rows, : 2 * rows].reshape(shard_count, 2, rows)
    gathered_vectors = gathered_vectors.transpose(1, 0, 2).reshape(2, shard_count * rows)
    return (
        gathered_matrix,
        gathered_vectors,
        master_rows,
        first_rows,
        second_rows,
        master_vecs,
        first_vecs,
        second_vecs,
    )


def solution(mesh):
    placed = (
        P(("rep", "shard"), None),
        P(("rep", "shard"), None),
        P(("rep", "shard"), None, None),
        P("shard", None),
        P("shard", None),
        P("shard", None),
        P(None, "shard"),
        P(None, "shard"),
        P(None, "shard"),
    )
    return jax.shard_map(
        per_device,
        mesh=mesh,
        in_specs=placed,
        out_specs=(
            P(),
            P(),
            P("shard", None),
            P("shard", None),
            P("shard", None),
            P(None, "shard"),
            P(None, "shard"),
            P(None, "shard"),
        ),
        check_vma=False,
    )
```

```python
import math

import jax
import jax.numpy as jnp
from jax import lax
from jax.sharding import PartitionSpec as P

beta_one = 0.9
beta_two = 0.95
adam_eps = 1e-08
decay_rate = 0.1
learn_rate = 0.2
bias_one = 0.9999734386011124
bias_two = 0.994079470779666
norm_eps = 1e-06


def moments(gradient, moment_one, moment_two):
    fresh_one = beta_one * moment_one + (1.0 - beta_one) * gradient
    fresh_two = beta_two * moment_two + (1.0 - beta_two) * gradient * gradient
    return (fresh_one, fresh_two)


def direction_of(fresh_one, fresh_two, master):
    return fresh_one / bias_one / (jnp.sqrt(fresh_two / bias_two) + adam_eps) + decay_rate * master


def _bit(value, k):
    return (value >> k) & 1


def _exchange(x, pairs):
    return lax.ppermute(x, ("rep", "shard"), pairs)


def _reduce_gradient(grad_term, rep_count, shard_count, rows):
    total = rep_count * shard_count
    chips = shard_count // 2
    width = grad_term.shape[1]
    rep_bits = rep_count.bit_length() - 1
    chip_bits = chips.bit_length() - 1
    slice_rows = rows // rep_count
    rep_idx = lax.axis_index("rep")
    shard_idx = lax.axis_index("shard")
    core = shard_idx % 2
    chip = shard_idx // 2

    def core_of(i):
        return (i % shard_count) % 2

    split = grad_term.reshape(chips, 2, rows, width)
    keep = lax.dynamic_index_in_dim(split, core, axis=1, keepdims=False)
    send = lax.dynamic_index_in_dim(split, 1 - core, axis=1, keepdims=False)
    held = keep + _exchange(send, [(i, i ^ 1) for i in range(total)])

    orders = (list(range(rep_bits)), list(reversed(range(rep_bits))))
    held = held.reshape(chips, rep_count, slice_rows, width)
    picks = []
    for j in range(rep_bits):
        pick = jnp.where(core == 0, _bit(rep_idx, orders[0][j]), _bit(rep_idx, orders[1][j]))
        picks.append(pick)
        pairs = [(i, i ^ ((1 << orders[core_of(i)][j]) * shard_count)) for i in range(total)]
        halves = held.reshape(chips, 2, -1, slice_rows, width)
        keep = lax.dynamic_index_in_dim(halves, pick, axis=1, keepdims=False)
        send = lax.dynamic_index_in_dim(halves, 1 - pick, axis=1, keepdims=False)
        held = keep + _exchange(send, pairs)
    held = held.reshape(chips, slice_rows, width)

    for j in range(chip_bits):
        pick = _bit(chip, j)
        pairs = [(i, i ^ ((1 << j) * 2)) for i in range(total)]
        halves = held.reshape(chips >> (j + 1), 2, slice_rows, width)
        keep = lax.dynamic_index_in_dim(halves, pick, axis=1, keepdims=False)
        send = lax.dynamic_index_in_dim(halves, 1 - pick, axis=1, keepdims=False)
        held = keep + _exchange(send, pairs)
    held = held.reshape(slice_rows, width)

    for j in reversed(range(rep_bits)):
        pick = picks[j]
        pairs = [(i, i ^ ((1 << orders[core_of(i)][j]) * shard_count)) for i in range(total)]
        other = _exchange(held, pairs)
        low = jnp.where(pick == 0, held, other)
        high = jnp.where(pick == 0, other, held)
        held = jnp.concatenate([low[None], high[None]], axis=0).reshape(-1, width)
    return held


def _sum_over_shard(values, shard_count, rep_count):
    total = rep_count * shard_count
    for j in range(shard_count.bit_length() - 1):
        values = values + _exchange(values, [(i, i ^ (1 << j)) for i in range(total)])
    return values


def per_device(
    activations,
    cotangents,
    grad_vectors,
    master_matrix,
    first_matrix,
    second_matrix,
    master_vector,
    first_vector,
    second_vector,
):
    rep_count = lax.axis_size("rep")
    shard_count = lax.axis_size("shard")
    tok_count, model_width = activations.shape
    rows = master_matrix.shape[0]
    grad_scale = 1.0 / math.sqrt(tok_count * rep_count * shard_count)
    shard_idx = lax.axis_index("shard")
    vector_term = grad_vectors[0].astype(jnp.float32) * grad_scale
    vector_sum = lax.psum(vector_term, ("rep", "shard"))
    weight_sq = jnp.sum(master_matrix * master_matrix)
    vector_sq = jnp.sum(master_vector * master_vector, axis=1)
    contract = (((0,), (0,)), ((), ()))
    grad_term = (
        lax.dot_general(cotangents, activations, contract, preferred_element_type=jnp.float32)
        * grad_scale
    )
    grad_rows = _reduce_gradient(grad_term, rep_count, shard_count, rows)
    grad_vecs = lax.dynamic_slice_in_dim(vector_sum, shard_idx * rows, rows, axis=1)
    first_rows, second_rows = moments(grad_rows, first_matrix, second_matrix)
    first_vecs, second_vecs = moments(grad_vecs, first_vector, second_vector)
    update_matrix = direction_of(first_rows, second_rows, master_matrix)
    update_vec = direction_of(first_vecs, second_vecs, master_vector)
    update_sq = jnp.sum(update_matrix * update_matrix)
    upvector_sq = jnp.sum(update_vec * update_vec, axis=1)
    sums = jnp.concatenate(
        [weight_sq[None], vector_sq, update_sq[None], upvector_sq]
    )
    sums = _sum_over_shard(sums, shard_count, rep_count)
    weight_tot, vector_tot, update_tot, upvector_tot = sums[0], sums[1:3], sums[3], sums[4:6]
    trust_matrix = jnp.sqrt(weight_tot) / jnp.sqrt(update_tot + norm_eps)
    trust_vec = (jnp.sqrt(vector_tot) / jnp.sqrt(upvector_tot + norm_eps))[:, None]
    stepped = master_matrix - learn_rate * trust_matrix * update_matrix
    master_rows = stepped / jnp.sqrt(jnp.mean(stepped * stepped, axis=1, keepdims=True) + norm_eps)
    master_vecs = master_vector - learn_rate * trust_vec * update_vec
    vec_row = master_vecs.astype(jnp.bfloat16).reshape(1, 2 * rows)
    vec_row = jnp.pad(vec_row, ((0, 15), (0, model_width - 2 * rows)))
    send = jnp.concatenate([master_rows.astype(jnp.bfloat16), vec_row], axis=0)
    gathered = lax.all_gather(send, "shard", axis=0, tiled=True)
    gathered = gathered.reshape(shard_count, rows + 16, model_width)
    gathered_matrix = gathered[:, :rows].reshape(shard_count * rows, model_width)
    gathered_vectors = gathered[:, rows, : 2 * rows].reshape(shard_count, 2, rows)
    gathered_vectors = gathered_vectors.transpose(1, 0, 2).reshape(2, shard_count * rows)
    return (
        gathered_matrix,
        gathered_vectors,
        master_rows,
        first_rows,
        second_rows,
        master_vecs,
        first_vecs,
        second_vecs,
    )


def solution(mesh):
    placed = (
        P(("rep", "shard"), None),
        P(("rep", "shard"), None),
        P(("rep", "shard"), None, None),
        P("shard", None),
        P("shard", None),
        P("shard", None),
        P(None, "shard"),
        P(None, "shard"),
        P(None, "shard"),
    )
    return jax.shard_map(
        per_device,
        mesh=mesh,
        in_specs=placed,
        out_specs=(
            P(),
            P(),
            P("shard", None),
            P("shard", None),
            P("shard", None),
            P(None, "shard"),
            P(None, "shard"),
            P(None, "shard"),
        ),
        check_vma=False,
    )
```

```python
import math

import jax
import jax.numpy as jnp
from jax import lax
from jax.sharding import PartitionSpec as P

beta_one = 0.9
beta_two = 0.95
adam_eps = 1e-08
decay_rate = 0.1
learn_rate = 0.2
bias_one = 0.9999734386011124
bias_two = 0.994079470779666
norm_eps = 1e-06


def moments(gradient, moment_one, moment_two):
    fresh_one = beta_one * moment_one + (1.0 - beta_one) * gradient
    fresh_two = beta_two * moment_two + (1.0 - beta_two) * gradient * gradient
    return (fresh_one, fresh_two)


def direction_of(fresh_one, fresh_two, master):
    return fresh_one / bias_one / (jnp.sqrt(fresh_two / bias_two) + adam_eps) + decay_rate * master


def _bit(value, k):
    return (value >> k) & 1


def _exchange(x, pairs):
    return lax.ppermute(x, ("rep", "shard"), pairs)


def _reduce_gradient(grad_term, vector, rep_count, shard_count, rows):
    total = rep_count * shard_count
    chips = shard_count // 2
    width = grad_term.shape[1]
    rep_bits = rep_count.bit_length() - 1
    chip_bits = chips.bit_length() - 1
    slice_rows = rows // rep_count
    rep_idx = lax.axis_index("rep")
    shard_idx = lax.axis_index("shard")
    core = shard_idx % 2
    chip = shard_idx // 2

    def core_of(i):
        return (i % shard_count) % 2

    split = grad_term.reshape(chips, 2, rows, width)
    keep = lax.dynamic_index_in_dim(split, core, axis=1, keepdims=False)
    send = lax.dynamic_index_in_dim(split, 1 - core, axis=1, keepdims=False)
    other, vec_other = _exchange((send, vector), [(i, i ^ 1) for i in range(total)])
    held = keep + other
    vector = vector + vec_other

    orders = (list(range(rep_bits)), list(reversed(range(rep_bits))))
    held = held.reshape(chips, rep_count, slice_rows, width)
    picks = []
    for j in range(rep_bits):
        pick = jnp.where(core == 0, _bit(rep_idx, orders[0][j]), _bit(rep_idx, orders[1][j]))
        picks.append(pick)
        pairs = [(i, i ^ ((1 << orders[core_of(i)][j]) * shard_count)) for i in range(total)]
        halves = held.reshape(chips, 2, -1, slice_rows, width)
        keep = lax.dynamic_index_in_dim(halves, pick, axis=1, keepdims=False)
        send = lax.dynamic_index_in_dim(halves, 1 - pick, axis=1, keepdims=False)
        other, vec_other = _exchange((send, vector), pairs)
        held = keep + other
        vector = vector + vec_other
    held = held.reshape(chips, slice_rows, width)

    for j in range(chip_bits):
        pick = _bit(chip, j)
        pairs = [(i, i ^ ((1 << j) * 2)) for i in range(total)]
        halves = held.reshape(chips >> (j + 1), 2, slice_rows, width)
        keep = lax.dynamic_index_in_dim(halves, pick, axis=1, keepdims=False)
        send = lax.dynamic_index_in_dim(halves, 1 - pick, axis=1, keepdims=False)
        other, vec_other = _exchange((send, vector), pairs)
        held = keep + other
        vector = vector + vec_other
    held = held.reshape(slice_rows, width)

    for j in reversed(range(rep_bits)):
        pick = picks[j]
        pairs = [(i, i ^ ((1 << orders[core_of(i)][j]) * shard_count)) for i in range(total)]
        other = _exchange(held, pairs)
        low = jnp.where(pick == 0, held, other)
        high = jnp.where(pick == 0, other, held)
        held = jnp.concatenate([low[None], high[None]], axis=0).reshape(-1, width)
    return held, vector


def _sum_over_shard(values, shard_count, rep_count):
    total = rep_count * shard_count
    for j in range(shard_count.bit_length() - 1):
        values = values + _exchange(values, [(i, i ^ (1 << j)) for i in range(total)])
    return values


def _gather_over_shard(values, shard_count, rep_count):
    total = rep_count * shard_count
    shard_idx = lax.axis_index("shard")
    held = values[None]
    for j in range(shard_count.bit_length() - 1):
        other = _exchange(held, [(i, i ^ (1 << j)) for i in range(total)])
        mine_low = _bit(shard_idx, j) == 0
        low = jnp.where(mine_low, held, other)
        high = jnp.where(mine_low, other, held)
        held = jnp.concatenate([low, high], axis=0)
    return held


def per_device(
    activations,
    cotangents,
    grad_vectors,
    master_matrix,
    first_matrix,
    second_matrix,
    master_vector,
    first_vector,
    second_vector,
):
    rep_count = lax.axis_size("rep")
    shard_count = lax.axis_size("shard")
    tok_count, model_width = activations.shape
    rows = master_matrix.shape[0]
    grad_scale = 1.0 / math.sqrt(tok_count * rep_count * shard_count)
    shard_idx = lax.axis_index("shard")
    vector_term = grad_vectors[0].astype(jnp.float32) * grad_scale
    weight_sq = jnp.sum(master_matrix * master_matrix)
    vector_sq = jnp.sum(master_vector * master_vector, axis=1)
    contract = (((0,), (0,)), ((), ()))
    grad_term = (
        lax.dot_general(cotangents, activations, contract, preferred_element_type=jnp.float32)
        * grad_scale
    )
    grad_rows, vector_sum = _reduce_gradient(grad_term, vector_term, rep_count, shard_count, rows)
    grad_vecs = lax.dynamic_slice_in_dim(vector_sum, shard_idx * rows, rows, axis=1)
    first_rows, second_rows = moments(grad_rows, first_matrix, second_matrix)
    first_vecs, second_vecs = moments(grad_vecs, first_vector, second_vector)
    update_matrix = direction_of(first_rows, second_rows, master_matrix)
    update_vec = direction_of(first_vecs, second_vecs, master_vector)
    update_sq = jnp.sum(update_matrix * update_matrix)
    upvector_sq = jnp.sum(update_vec * update_vec, axis=1)
    sums = jnp.concatenate(
        [weight_sq[None], vector_sq, update_sq[None], upvector_sq]
    )
    sums = _sum_over_shard(sums, shard_count, rep_count)
    weight_tot, vector_tot, update_tot, upvector_tot = sums[0], sums[1:3], sums[3], sums[4:6]
    trust_matrix = jnp.sqrt(weight_tot) / jnp.sqrt(update_tot + norm_eps)
    trust_vec = (jnp.sqrt(vector_tot) / jnp.sqrt(upvector_tot + norm_eps))[:, None]
    stepped = master_matrix - learn_rate * trust_matrix * update_matrix
    master_rows = stepped / jnp.sqrt(jnp.mean(stepped * stepped, axis=1, keepdims=True) + norm_eps)
    master_vecs = master_vector - learn_rate * trust_vec * update_vec
    gathered_matrix = lax.all_gather(
        master_rows.astype(jnp.bfloat16), "shard", axis=0, tiled=True
    )
    gathered_vectors = _gather_over_shard(master_vecs.astype(jnp.bfloat16), shard_count, rep_count)
    gathered_vectors = gathered_vectors.transpose(1, 0, 2).reshape(2, shard_count * rows)
    return (
        gathered_matrix,
        gathered_vectors,
        master_rows,
        first_rows,
        second_rows,
        master_vecs,
        first_vecs,
        second_vecs,
    )


def solution(mesh):
    placed = (
        P(("rep", "shard"), None),
        P(("rep", "shard"), None),
        P(("rep", "shard"), None, None),
        P("shard", None),
        P("shard", None),
        P("shard", None),
        P(None, "shard"),
        P(None, "shard"),
        P(None, "shard"),
    )
    return jax.shard_map(
        per_device,
        mesh=mesh,
        in_specs=placed,
        out_specs=(
            P(),
            P(),
            P("shard", None),
            P("shard", None),
            P("shard", None),
            P(None, "shard"),
            P(None, "shard"),
            P(None, "shard"),
        ),
        check_vma=False,
    )
```

```python
import math

import jax
import jax.numpy as jnp
from jax import lax
from jax.sharding import PartitionSpec as P

beta_one = 0.9
beta_two = 0.95
adam_eps = 1e-08
decay_rate = 0.1
learn_rate = 0.2
bias_one = 0.9999734386011124
bias_two = 0.994079470779666
norm_eps = 1e-06


def moments(gradient, moment_one, moment_two):
    fresh_one = beta_one * moment_one + (1.0 - beta_one) * gradient
    fresh_two = beta_two * moment_two + (1.0 - beta_two) * gradient * gradient
    return (fresh_one, fresh_two)


def direction_of(fresh_one, fresh_two, master):
    return fresh_one / bias_one / (jnp.sqrt(fresh_two / bias_two) + adam_eps) + decay_rate * master


def _bit(value, k):
    return (value >> k) & 1


def _exchange(x, pairs):
    return lax.ppermute(x, ("rep", "shard"), pairs)


def _with_vector(block, vector):
    width = block.shape[-1]
    pad = jnp.zeros((8 - vector.shape[0], width), vector.dtype)
    return jnp.concatenate([block.reshape(-1, width), vector, pad], axis=0)


def _swap(block, vector, pairs):
    got = _exchange(_with_vector(block, vector), pairs)
    size = block.size // block.shape[-1]
    return got[:size].reshape(block.shape), got[size : size + vector.shape[0]]


def _reduce_gradient(cotangents, activations, grad_scale, vector, rep_count, shard_count, rows):
    total = rep_count * shard_count
    chips = shard_count // 2
    tok_count, width = activations.shape
    rep_bits = rep_count.bit_length() - 1
    chip_bits = chips.bit_length() - 1
    slice_rows = rows // rep_count
    rep_idx = lax.axis_index("rep")
    shard_idx = lax.axis_index("shard")
    core = shard_idx % 2
    chip = shard_idx // 2
    contract = (((0,), (0,)), ((), ()))

    def core_of(i):
        return (i % shard_count) % 2

    def rows_of(parity):
        picked = lax.dynamic_index_in_dim(
            cotangents.reshape(tok_count, chips, 2, rows), parity, axis=2, keepdims=False
        ).reshape(tok_count, chips * rows)
        product = lax.dot_general(picked, activations, contract, preferred_element_type=jnp.float32)
        return (product * grad_scale).reshape(chips, rows, width)

    send = rows_of(1 - core)
    other, vec_other = _swap(send, vector, [(i, i ^ 1) for i in range(total)])
    held = lax.optimization_barrier(rows_of(core)) + other
    vector = vector + vec_other

    orders = (list(range(rep_bits)), list(reversed(range(rep_bits))))
    held = held.reshape(chips, rep_count, slice_rows, width)
    picks = []
    for j in range(rep_bits):
        pick = jnp.where(core == 0, _bit(rep_idx, orders[0][j]), _bit(rep_idx, orders[1][j]))
        picks.append(pick)
        pairs = [(i, i ^ ((1 << orders[core_of(i)][j]) * shard_count)) for i in range(total)]
        halves = held.reshape(chips, 2, -1, slice_rows, width)
        keep = lax.dynamic_index_in_dim(halves, pick, axis=1, keepdims=False)
        send = lax.dynamic_index_in_dim(halves, 1 - pick, axis=1, keepdims=False)
        other, vec_other = _swap(send, vector, pairs)
        held = keep + other
        vector = vector + vec_other
    held = held.reshape(chips, slice_rows, width)

    for j in range(chip_bits):
        pick = _bit(chip, j)
        pairs = [(i, i ^ ((1 << j) * 2)) for i in range(total)]
        halves = held.reshape(chips >> (j + 1), 2, slice_rows, width)
        keep = lax.dynamic_index_in_dim(halves, pick, axis=1, keepdims=False)
        send = lax.dynamic_index_in_dim(halves, 1 - pick, axis=1, keepdims=False)
        other, vec_other = _swap(send, vector, pairs)
        held = keep + other
        vector = vector + vec_other
    held = held.reshape(slice_rows, width)

    for j in reversed(range(rep_bits)):
        pick = picks[j]
        pairs = [(i, i ^ ((1 << orders[core_of(i)][j]) * shard_count)) for i in range(total)]
        other = _exchange(held, pairs)
        low = jnp.where(pick == 0, held, other)
        high = jnp.where(pick == 0, other, held)
        held = jnp.concatenate([low[None], high[None]], axis=0).reshape(-1, width)
    return held, vector


def _sum_over_shard(values, shard_count, rep_count):
    total = rep_count * shard_count
    for j in range(shard_count.bit_length() - 1):
        values = values + _exchange(values, [(i, i ^ (1 << j)) for i in range(total)])
    return values


def _gather_over_shard(values, shard_count, rep_count):
    total = rep_count * shard_count
    shard_idx = lax.axis_index("shard")
    held = values[None]
    for j in range(shard_count.bit_length() - 1):
        other = _exchange(held, [(i, i ^ (1 << j)) for i in range(total)])
        mine_low = _bit(shard_idx, j) == 0
        low = jnp.where(mine_low, held, other)
        high = jnp.where(mine_low, other, held)
        held = jnp.concatenate([low, high], axis=0)
    return held


def per_device(
    activations,
    cotangents,
    grad_vectors,
    master_matrix,
    first_matrix,
    second_matrix,
    master_vector,
    first_vector,
    second_vector,
):
    rep_count = lax.axis_size("rep")
    shard_count = lax.axis_size("shard")
    tok_count, model_width = activations.shape
    rows = master_matrix.shape[0]
    grad_scale = 1.0 / math.sqrt(tok_count * rep_count * shard_count)
    shard_idx = lax.axis_index("shard")
    vector_term = grad_vectors[0].astype(jnp.float32) * grad_scale
    weight_sq = jnp.sum(master_matrix * master_matrix)
    vector_sq = jnp.sum(master_vector * master_vector, axis=1)
    grad_rows, vector_sum = _reduce_gradient(
        cotangents, activations, grad_scale, vector_term, rep_count, shard_count, rows
    )
    grad_vecs = lax.dynamic_slice_in_dim(vector_sum, shard_idx * rows, rows, axis=1)
    first_rows, second_rows = moments(grad_rows, first_matrix, second_matrix)
    first_vecs, second_vecs = moments(grad_vecs, first_vector, second_vector)
    update_matrix = direction_of(first_rows, second_rows, master_matrix)
    update_vec = direction_of(first_vecs, second_vecs, master_vector)
    update_sq = jnp.sum(update_matrix * update_matrix)
    upvector_sq = jnp.sum(update_vec * update_vec, axis=1)
    sums = jnp.concatenate(
        [weight_sq[None], vector_sq, update_sq[None], upvector_sq]
    )
    sums = _sum_over_shard(sums, shard_count, rep_count)
    weight_tot, vector_tot, update_tot, upvector_tot = sums[0], sums[1:3], sums[3], sums[4:6]
    trust_matrix = jnp.sqrt(weight_tot) / jnp.sqrt(update_tot + norm_eps)
    trust_vec = (jnp.sqrt(vector_tot) / jnp.sqrt(upvector_tot + norm_eps))[:, None]
    stepped = master_matrix - learn_rate * trust_matrix * update_matrix
    master_rows = stepped / jnp.sqrt(jnp.mean(stepped * stepped, axis=1, keepdims=True) + norm_eps)
    master_vecs = master_vector - learn_rate * trust_vec * update_vec
    gathered_matrix = lax.all_gather(
        master_rows.astype(jnp.bfloat16), "shard", axis=0, tiled=True
    )
    gathered_vectors = _gather_over_shard(master_vecs.astype(jnp.bfloat16), shard_count, rep_count)
    gathered_vectors = gathered_vectors.transpose(1, 0, 2).reshape(2, shard_count * rows)
    return (
        gathered_matrix,
        gathered_vectors,
        master_rows,
        first_rows,
        second_rows,
        master_vecs,
        first_vecs,
        second_vecs,
    )


def solution(mesh):
    placed = (
        P(("rep", "shard"), None),
        P(("rep", "shard"), None),
        P(("rep", "shard"), None, None),
        P("shard", None),
        P("shard", None),
        P("shard", None),
        P(None, "shard"),
        P(None, "shard"),
        P(None, "shard"),
    )
    return jax.shard_map(
        per_device,
        mesh=mesh,
        in_specs=placed,
        out_specs=(
            P(),
            P(),
            P("shard", None),
            P("shard", None),
            P("shard", None),
            P(None, "shard"),
            P(None, "shard"),
            P(None, "shard"),
        ),
        check_vma=False,
    )
```

```python
import math

import jax
import jax.numpy as jnp
from jax import lax
from jax.sharding import PartitionSpec as P

beta_one = 0.9
beta_two = 0.95
adam_eps = 1e-08
decay_rate = 0.1
learn_rate = 0.2
bias_one = 0.9999734386011124
bias_two = 0.994079470779666
norm_eps = 1e-06


def moments(gradient, moment_one, moment_two):
    fresh_one = beta_one * moment_one + (1.0 - beta_one) * gradient
    fresh_two = beta_two * moment_two + (1.0 - beta_two) * gradient * gradient
    return (fresh_one, fresh_two)


def direction_of(fresh_one, fresh_two, master):
    return fresh_one / bias_one / (jnp.sqrt(fresh_two / bias_two) + adam_eps) + decay_rate * master


def _bit(value, k):
    return (value >> k) & 1


def _exchange(x, pairs):
    return lax.ppermute(x, ("rep", "shard"), pairs)


def _with_vector(block, vector):
    width = block.shape[-1]
    pad = jnp.zeros((8 - vector.shape[0], width), vector.dtype)
    return jnp.concatenate([block.reshape(-1, width), vector, pad], axis=0)


def _swap(block, vector, pairs):
    got = _exchange(_with_vector(block, vector), pairs)
    size = block.size // block.shape[-1]
    return got[:size].reshape(block.shape), got[size : size + vector.shape[0]]


def _reduce_gradient(cotangents, activations, grad_scale, vector, rep_count, shard_count, rows):
    total = rep_count * shard_count
    chips = shard_count // 2
    tok_count, width = activations.shape
    rep_bits = rep_count.bit_length() - 1
    chip_bits = chips.bit_length() - 1
    slice_rows = rows // rep_count
    rep_idx = lax.axis_index("rep")
    shard_idx = lax.axis_index("shard")
    core = shard_idx % 2
    chip = shard_idx // 2
    contract = (((0,), (0,)), ((), ()))

    def core_of(i):
        return (i % shard_count) % 2

    grad_term = (
        lax.dot_general(cotangents, activations, contract, preferred_element_type=jnp.float32)
        * grad_scale
    )

    split = grad_term.reshape(chips, 2, rows, width)
    keep = lax.dynamic_index_in_dim(split, core, axis=1, keepdims=False)
    send = lax.dynamic_index_in_dim(split, 1 - core, axis=1, keepdims=False)
    other, vec_other = _swap(send, vector, [(i, i ^ 1) for i in range(total)])
    held = keep + other
    vector = vector + vec_other

    orders = (list(range(rep_bits)), list(reversed(range(rep_bits))))
    held = held.reshape(chips, rep_count, slice_rows, width)
    picks = []
    for j in range(rep_bits):
        pick = jnp.where(core == 0, _bit(rep_idx, orders[0][j]), _bit(rep_idx, orders[1][j]))
        picks.append(pick)
        pairs = [(i, i ^ ((1 << orders[core_of(i)][j]) * shard_count)) for i in range(total)]
        halves = held.reshape(chips, 2, -1, slice_rows, width)
        keep = lax.dynamic_index_in_dim(halves, pick, axis=1, keepdims=False)
        send = lax.dynamic_index_in_dim(halves, 1 - pick, axis=1, keepdims=False)
        other, vec_other = _swap(send, vector, pairs)
        held = keep + other
        vector = vector + vec_other
    held = held.reshape(chips, slice_rows, width)

    for j in range(chip_bits):
        pick = _bit(chip, j)
        pairs = [(i, i ^ ((1 << j) * 2)) for i in range(total)]
        halves = held.reshape(chips >> (j + 1), 2, slice_rows, width)
        keep = lax.dynamic_index_in_dim(halves, pick, axis=1, keepdims=False)
        send = lax.dynamic_index_in_dim(halves, 1 - pick, axis=1, keepdims=False)
        other, vec_other = _swap(send, vector, pairs)
        held = keep + other
        vector = vector + vec_other
    held = held.reshape(slice_rows, width)

    for j in reversed(range(rep_bits)):
        pick = picks[j]
        pairs = [(i, i ^ ((1 << orders[core_of(i)][j]) * shard_count)) for i in range(total)]
        other = _exchange(held, pairs)
        low = jnp.where(pick == 0, held, other)
        high = jnp.where(pick == 0, other, held)
        held = jnp.concatenate([low[None], high[None]], axis=0).reshape(-1, width)
    return held, vector


def _sum_over_shard(values, shard_count, rep_count):
    total = rep_count * shard_count
    for j in range(shard_count.bit_length() - 1):
        values = values + _exchange(values, [(i, i ^ (1 << j)) for i in range(total)])
    return values


def _gather_over_shard(values, shard_count, rep_count):
    total = rep_count * shard_count
    shard_idx = lax.axis_index("shard")
    held = values[None]
    for j in range(shard_count.bit_length() - 1):
        other = _exchange(held, [(i, i ^ (1 << j)) for i in range(total)])
        mine_low = _bit(shard_idx, j) == 0
        low = jnp.where(mine_low, held, other)
        high = jnp.where(mine_low, other, held)
        held = jnp.concatenate([low, high], axis=0)
    return held


def per_device(
    activations,
    cotangents,
    grad_vectors,
    master_matrix,
    first_matrix,
    second_matrix,
    master_vector,
    first_vector,
    second_vector,
):
    rep_count = lax.axis_size("rep")
    shard_count = lax.axis_size("shard")
    tok_count, model_width = activations.shape
    rows = master_matrix.shape[0]
    grad_scale = 1.0 / math.sqrt(tok_count * rep_count * shard_count)
    shard_idx = lax.axis_index("shard")
    vector_term = grad_vectors[0].astype(jnp.float32) * grad_scale
    weight_sq = jnp.sum(master_matrix * master_matrix)
    vector_sq = jnp.sum(master_vector * master_vector, axis=1)
    grad_rows, vector_sum = _reduce_gradient(
        cotangents, activations, grad_scale, vector_term, rep_count, shard_count, rows
    )
    grad_vecs = lax.dynamic_slice_in_dim(vector_sum, shard_idx * rows, rows, axis=1)
    first_rows, second_rows = moments(grad_rows, first_matrix, second_matrix)
    first_vecs, second_vecs = moments(grad_vecs, first_vector, second_vector)
    update_matrix = direction_of(first_rows, second_rows, master_matrix)
    update_vec = direction_of(first_vecs, second_vecs, master_vector)
    update_sq = jnp.sum(update_matrix * update_matrix)
    upvector_sq = jnp.sum(update_vec * update_vec, axis=1)
    sums = jnp.concatenate(
        [weight_sq[None], vector_sq, update_sq[None], upvector_sq]
    )
    sums = _sum_over_shard(sums, shard_count, rep_count)
    weight_tot, vector_tot, update_tot, upvector_tot = sums[0], sums[1:3], sums[3], sums[4:6]
    trust_matrix = jnp.sqrt(weight_tot) / jnp.sqrt(update_tot + norm_eps)
    trust_vec = (jnp.sqrt(vector_tot) / jnp.sqrt(upvector_tot + norm_eps))[:, None]
    stepped = master_matrix - learn_rate * trust_matrix * update_matrix
    master_rows = stepped / jnp.sqrt(jnp.mean(stepped * stepped, axis=1, keepdims=True) + norm_eps)
    master_vecs = master_vector - learn_rate * trust_vec * update_vec
    gathered_matrix = lax.all_gather(
        master_rows.astype(jnp.bfloat16), "shard", axis=0, tiled=True
    )
    gathered_vectors = _gather_over_shard(master_vecs.astype(jnp.bfloat16), shard_count, rep_count)
    gathered_vectors = gathered_vectors.transpose(1, 0, 2).reshape(2, shard_count * rows)
    return (
        gathered_matrix,
        gathered_vectors,
        master_rows,
        first_rows,
        second_rows,
        master_vecs,
        first_vecs,
        second_vecs,
    )


def solution(mesh):
    placed = (
        P(("rep", "shard"), None),
        P(("rep", "shard"), None),
        P(("rep", "shard"), None, None),
        P("shard", None),
        P("shard", None),
        P("shard", None),
        P(None, "shard"),
        P(None, "shard"),
        P(None, "shard"),
    )
    return jax.shard_map(
        per_device,
        mesh=mesh,
        in_specs=placed,
        out_specs=(
            P(),
            P(),
            P("shard", None),
            P("shard", None),
            P("shard", None),
            P(None, "shard"),
            P(None, "shard"),
            P(None, "shard"),
        ),
        check_vma=False,
    )
```

```python
import math

import jax
import jax.numpy as jnp
from jax import lax
from jax.sharding import PartitionSpec as P

beta_one = 0.9
beta_two = 0.95
adam_eps = 1e-08
decay_rate = 0.1
learn_rate = 0.2
bias_one = 0.9999734386011124
bias_two = 0.994079470779666
norm_eps = 1e-06


def moments(gradient, moment_one, moment_two):
    fresh_one = beta_one * moment_one + (1.0 - beta_one) * gradient
    fresh_two = beta_two * moment_two + (1.0 - beta_two) * gradient * gradient
    return (fresh_one, fresh_two)


def direction_of(fresh_one, fresh_two, master):
    return fresh_one / bias_one / (jnp.sqrt(fresh_two / bias_two) + adam_eps) + decay_rate * master


def _bit(value, k):
    return (value >> k) & 1


def _exchange(x, pairs):
    return lax.ppermute(x, ("rep", "shard"), pairs)


def _swap(block, vector, pairs):
    other, vec_other = _exchange((block, vector), pairs)
    return lax.optimization_barrier((other, vec_other))


def _reduce_gradient(cotangents, activations, grad_scale, vector, rep_count, shard_count, rows):
    total = rep_count * shard_count
    chips = shard_count // 2
    tok_count, width = activations.shape
    half = width // 2
    rep_bits = rep_count.bit_length() - 1
    chip_bits = chips.bit_length() - 1
    slice_rows = rows // rep_count
    rep_idx = lax.axis_index("rep")
    shard_idx = lax.axis_index("shard")
    core = shard_idx % 2
    chip = shard_idx // 2
    contract = (((0,), (0,)), ((), ()))

    def core_of(i):
        return (i % shard_count) % 2

    def columns_of(part):
        picked = lax.dynamic_slice_in_dim(activations, part * half, half, axis=1)
        product = lax.dot_general(cotangents, picked, contract, preferred_element_type=jnp.float32)
        return product * grad_scale

    send = columns_of(1 - core)
    other, vec_other = _swap(send, vector, [(i, i ^ 1) for i in range(total)])
    held = lax.optimization_barrier(columns_of(core)) + other
    vector = vector + vec_other

    orders = (list(range(rep_bits)), list(reversed(range(rep_bits))))
    held = held.reshape(chips * 2, rep_count, slice_rows, half)
    picks = []
    for j in range(rep_bits):
        pick = jnp.where(core == 0, _bit(rep_idx, orders[0][j]), _bit(rep_idx, orders[1][j]))
        picks.append(pick)
        pairs = [(i, i ^ ((1 << orders[core_of(i)][j]) * shard_count)) for i in range(total)]
        halves = held.reshape(chips * 2, 2, -1, slice_rows, half)
        keep = lax.dynamic_index_in_dim(halves, pick, axis=1, keepdims=False)
        send = lax.dynamic_index_in_dim(halves, 1 - pick, axis=1, keepdims=False)
        other, vec_other = _swap(send, vector, pairs)
        held = keep + other
        vector = vector + vec_other
    held = held.reshape(chips, 2, slice_rows, half)

    for j in range(chip_bits):
        pick = _bit(chip, j)
        pairs = [(i, i ^ ((1 << j) * 2)) for i in range(total)]
        halves = held.reshape(chips >> (j + 1), 2, 2, slice_rows, half)
        keep = lax.dynamic_index_in_dim(halves, pick, axis=1, keepdims=False)
        send = lax.dynamic_index_in_dim(halves, 1 - pick, axis=1, keepdims=False)
        other, vec_other = _swap(send, vector, pairs)
        held = keep + other
        vector = vector + vec_other
    held = held.reshape(2, slice_rows, half)

    def reversed_rep(i):
        rep, shard = divmod(i, shard_count)
        flipped = int(format(rep, f"0{rep_bits}b")[::-1], 2) if rep_bits else 0
        return flipped * shard_count + (shard ^ 1)

    mine = lax.dynamic_index_in_dim(held, core, axis=0, keepdims=False)
    theirs = lax.dynamic_index_in_dim(held, 1 - core, axis=0, keepdims=False)
    got = _exchange(theirs, [(i, reversed_rep(i)) for i in range(total)])
    left = jnp.where(core == 0, mine, got)
    right = jnp.where(core == 0, got, mine)
    held = jnp.concatenate([left, right], axis=1)

    for j in reversed(range(rep_bits)):
        pick = picks[j]
        pairs = [(i, i ^ ((1 << orders[core_of(i)][j]) * shard_count)) for i in range(total)]
        other = _exchange(held, pairs)
        low = jnp.where(pick == 0, held, other)
        high = jnp.where(pick == 0, other, held)
        held = jnp.concatenate([low[None], high[None]], axis=0).reshape(-1, width)
    return held, vector


def _sum_over_shard(values, shard_count, rep_count):
    total = rep_count * shard_count
    for j in range(shard_count.bit_length() - 1):
        values = values + _exchange(values, [(i, i ^ (1 << j)) for i in range(total)])
    return values


def _gather_over_shard(values, shard_count, rep_count):
    total = rep_count * shard_count
    shard_idx = lax.axis_index("shard")
    held = values[None]
    for j in range(shard_count.bit_length() - 1):
        other = _exchange(held, [(i, i ^ (1 << j)) for i in range(total)])
        mine_low = _bit(shard_idx, j) == 0
        low = jnp.where(mine_low, held, other)
        high = jnp.where(mine_low, other, held)
        held = jnp.concatenate([low, high], axis=0)
    return held


def per_device(
    activations,
    cotangents,
    grad_vectors,
    master_matrix,
    first_matrix,
    second_matrix,
    master_vector,
    first_vector,
    second_vector,
):
    rep_count = lax.axis_size("rep")
    shard_count = lax.axis_size("shard")
    tok_count, model_width = activations.shape
    rows = master_matrix.shape[0]
    grad_scale = 1.0 / math.sqrt(tok_count * rep_count * shard_count)
    shard_idx = lax.axis_index("shard")
    vector_term = grad_vectors[0].astype(jnp.float32) * grad_scale
    weight_sq = jnp.sum(master_matrix * master_matrix)
    vector_sq = jnp.sum(master_vector * master_vector, axis=1)
    grad_rows, vector_sum = _reduce_gradient(
        cotangents, activations, grad_scale, vector_term, rep_count, shard_count, rows
    )
    grad_vecs = lax.dynamic_slice_in_dim(vector_sum, shard_idx * rows, rows, axis=1)
    first_rows, second_rows = moments(grad_rows, first_matrix, second_matrix)
    first_vecs, second_vecs = moments(grad_vecs, first_vector, second_vector)
    update_matrix = direction_of(first_rows, second_rows, master_matrix)
    update_vec = direction_of(first_vecs, second_vecs, master_vector)
    update_sq = jnp.sum(update_matrix * update_matrix)
    upvector_sq = jnp.sum(update_vec * update_vec, axis=1)
    sums = jnp.concatenate(
        [weight_sq[None], vector_sq, update_sq[None], upvector_sq]
    )
    sums = _sum_over_shard(sums, shard_count, rep_count)
    weight_tot, vector_tot, update_tot, upvector_tot = sums[0], sums[1:3], sums[3], sums[4:6]
    trust_matrix = jnp.sqrt(weight_tot) / jnp.sqrt(update_tot + norm_eps)
    trust_vec = (jnp.sqrt(vector_tot) / jnp.sqrt(upvector_tot + norm_eps))[:, None]
    stepped = master_matrix - learn_rate * trust_matrix * update_matrix
    master_rows = stepped / jnp.sqrt(jnp.mean(stepped * stepped, axis=1, keepdims=True) + norm_eps)
    master_vecs = master_vector - learn_rate * trust_vec * update_vec
    gathered_matrix = lax.all_gather(
        master_rows.astype(jnp.bfloat16), "shard", axis=0, tiled=True
    )
    gathered_vectors = _gather_over_shard(master_vecs.astype(jnp.bfloat16), shard_count, rep_count)
    gathered_vectors = gathered_vectors.transpose(1, 0, 2).reshape(2, shard_count * rows)
    return (
        gathered_matrix,
        gathered_vectors,
        master_rows,
        first_rows,
        second_rows,
        master_vecs,
        first_vecs,
        second_vecs,
    )


def solution(mesh):
    placed = (
        P(("rep", "shard"), None),
        P(("rep", "shard"), None),
        P(("rep", "shard"), None, None),
        P("shard", None),
        P("shard", None),
        P("shard", None),
        P(None, "shard"),
        P(None, "shard"),
        P(None, "shard"),
    )
    return jax.shard_map(
        per_device,
        mesh=mesh,
        in_specs=placed,
        out_specs=(
            P(),
            P(),
            P("shard", None),
            P("shard", None),
            P("shard", None),
            P(None, "shard"),
            P(None, "shard"),
            P(None, "shard"),
        ),
        check_vma=False,
    )
```

```python
import math

import jax
import jax.numpy as jnp
from jax import lax
from jax.sharding import PartitionSpec as P

beta_one = 0.9
beta_two = 0.95
adam_eps = 1e-08
decay_rate = 0.1
learn_rate = 0.2
bias_one = 0.9999734386011124
bias_two = 0.994079470779666
norm_eps = 1e-06


def moments(gradient, moment_one, moment_two):
    fresh_one = beta_one * moment_one + (1.0 - beta_one) * gradient
    fresh_two = beta_two * moment_two + (1.0 - beta_two) * gradient * gradient
    return (fresh_one, fresh_two)


def direction_of(fresh_one, fresh_two, master):
    return fresh_one / bias_one / (jnp.sqrt(fresh_two / bias_two) + adam_eps) + decay_rate * master


def _bit(value, k):
    return (value >> k) & 1


def _exchange(x, pairs):
    return lax.ppermute(x, ("rep", "shard"), pairs)


def _swap(block, vector, pairs):
    other, vec_other = _exchange((block, vector), pairs)
    return lax.optimization_barrier((other, vec_other))


def _reduce_gradient(cotangents, activations, grad_scale, vector, rep_count, shard_count, rows):
    total = rep_count * shard_count
    chips = shard_count // 2
    tok_count, width = activations.shape
    rep_bits = rep_count.bit_length() - 1
    chip_bits = chips.bit_length() - 1
    slice_rows = rows // rep_count
    rep_idx = lax.axis_index("rep")
    shard_idx = lax.axis_index("shard")
    core = shard_idx % 2
    chip = shard_idx // 2
    contract = (((0,), (0,)), ((), ()))

    def core_of(i):
        return (i % shard_count) % 2

    grad_term = (
        lax.dot_general(cotangents, activations, contract, preferred_element_type=jnp.float32)
        * grad_scale
    )

    split = grad_term.reshape(chips, 2, rows, width)
    keep = lax.dynamic_index_in_dim(split, core, axis=1, keepdims=False)
    send = lax.dynamic_index_in_dim(split, 1 - core, axis=1, keepdims=False)
    other, vec_other = _swap(send, vector, [(i, i ^ 1) for i in range(total)])
    held = keep + other
    vector = vector + vec_other

    orders = (list(range(rep_bits)), list(reversed(range(rep_bits))))
    held = held.reshape(chips, rep_count, slice_rows, width)
    picks = []
    for j in range(rep_bits):
        pick = jnp.where(core == 0, _bit(rep_idx, orders[0][j]), _bit(rep_idx, orders[1][j]))
        picks.append(pick)
        pairs = [(i, i ^ ((1 << orders[core_of(i)][j]) * shard_count)) for i in range(total)]
        halves = held.reshape(chips, 2, -1, slice_rows, width)
        keep = lax.dynamic_index_in_dim(halves, pick, axis=1, keepdims=False)
        send = lax.dynamic_index_in_dim(halves, 1 - pick, axis=1, keepdims=False)
        other, vec_other = _swap(send, vector, pairs)
        held = keep + other
        vector = vector + vec_other
    held = held.reshape(chips, slice_rows, width)

    for j in range(chip_bits):
        pick = _bit(chip, j)
        pairs = [(i, i ^ ((1 << j) * 2)) for i in range(total)]
        halves = held.reshape(chips >> (j + 1), 2, slice_rows, width)
        keep = lax.dynamic_index_in_dim(halves, pick, axis=1, keepdims=False)
        send = lax.dynamic_index_in_dim(halves, 1 - pick, axis=1, keepdims=False)
        other, vec_other = _swap(send, vector, pairs)
        held = keep + other
        vector = vector + vec_other
    held = held.reshape(slice_rows, width)

    for j in reversed(range(rep_bits)):
        pick = picks[j]
        pairs = [(i, i ^ ((1 << orders[core_of(i)][j]) * shard_count)) for i in range(total)]
        other = _exchange(held, pairs)
        low = jnp.where(pick == 0, held, other)
        high = jnp.where(pick == 0, other, held)
        held = jnp.concatenate([low[None], high[None]], axis=0).reshape(-1, width)
    return held, vector


def _sum_over_shard(values, shard_count, rep_count):
    total = rep_count * shard_count
    for j in range(shard_count.bit_length() - 1):
        values = values + _exchange(values, [(i, i ^ (1 << j)) for i in range(total)])
    return values


def _gather_over_shard(values, shard_count, rep_count):
    total = rep_count * shard_count
    shard_idx = lax.axis_index("shard")
    held = values[None]
    for j in range(shard_count.bit_length() - 1):
        other = _exchange(held, [(i, i ^ (1 << j)) for i in range(total)])
        mine_low = _bit(shard_idx, j) == 0
        low = jnp.where(mine_low, held, other)
        high = jnp.where(mine_low, other, held)
        held = jnp.concatenate([low, high], axis=0)
    return held


def per_device(
    activations,
    cotangents,
    grad_vectors,
    master_matrix,
    first_matrix,
    second_matrix,
    master_vector,
    first_vector,
    second_vector,
):
    rep_count = lax.axis_size("rep")
    shard_count = lax.axis_size("shard")
    tok_count, model_width = activations.shape
    rows = master_matrix.shape[0]
    grad_scale = 1.0 / math.sqrt(tok_count * rep_count * shard_count)
    shard_idx = lax.axis_index("shard")
    vector_term = grad_vectors[0].astype(jnp.float32) * grad_scale
    weight_sq = jnp.sum(master_matrix * master_matrix)
    vector_sq = jnp.sum(master_vector * master_vector, axis=1)
    grad_rows, vector_sum = _reduce_gradient(
        cotangents, activations, grad_scale, vector_term, rep_count, shard_count, rows
    )
    grad_vecs = lax.dynamic_slice_in_dim(vector_sum, shard_idx * rows, rows, axis=1)
    first_rows, second_rows = moments(grad_rows, first_matrix, second_matrix)
    first_vecs, second_vecs = moments(grad_vecs, first_vector, second_vector)
    update_matrix = direction_of(first_rows, second_rows, master_matrix)
    update_vec = direction_of(first_vecs, second_vecs, master_vector)
    update_sq = jnp.sum(update_matrix * update_matrix)
    upvector_sq = jnp.sum(update_vec * update_vec, axis=1)
    sums = jnp.concatenate(
        [weight_sq[None], vector_sq, update_sq[None], upvector_sq]
    )
    sums = _sum_over_shard(sums, shard_count, rep_count)
    weight_tot, vector_tot, update_tot, upvector_tot = sums[0], sums[1:3], sums[3], sums[4:6]
    trust_matrix = jnp.sqrt(weight_tot) / jnp.sqrt(update_tot + norm_eps)
    trust_vec = (jnp.sqrt(vector_tot) / jnp.sqrt(upvector_tot + norm_eps))[:, None]
    stepped = master_matrix - learn_rate * trust_matrix * update_matrix
    master_rows = stepped / jnp.sqrt(jnp.mean(stepped * stepped, axis=1, keepdims=True) + norm_eps)
    master_vecs = master_vector - learn_rate * trust_vec * update_vec
    gathered_matrix = lax.all_gather(
        master_rows.astype(jnp.bfloat16), "shard", axis=0, tiled=True
    )
    gathered_vectors = _gather_over_shard(master_vecs.astype(jnp.bfloat16), shard_count, rep_count)
    gathered_vectors = gathered_vectors.transpose(1, 0, 2).reshape(2, shard_count * rows)
    return (
        gathered_matrix,
        gathered_vectors,
        master_rows,
        first_rows,
        second_rows,
        master_vecs,
        first_vecs,
        second_vecs,
    )


def solution(mesh):
    placed = (
        P(("rep", "shard"), None),
        P(("rep", "shard"), None),
        P(("rep", "shard"), None, None),
        P("shard", None),
        P("shard", None),
        P("shard", None),
        P(None, "shard"),
        P(None, "shard"),
        P(None, "shard"),
    )
    return jax.shard_map(
        per_device,
        mesh=mesh,
        in_specs=placed,
        out_specs=(
            P(),
            P(),
            P("shard", None),
            P("shard", None),
            P("shard", None),
            P(None, "shard"),
            P(None, "shard"),
            P(None, "shard"),
        ),
        check_vma=False,
    )
```

```python
import math

import jax
import jax.numpy as jnp
from jax import lax
from jax.sharding import PartitionSpec as P

beta_one = 0.9
beta_two = 0.95
adam_eps = 1e-08
decay_rate = 0.1
learn_rate = 0.2
bias_one = 0.9999734386011124
bias_two = 0.994079470779666
norm_eps = 1e-06


def moments(gradient, moment_one, moment_two):
    fresh_one = beta_one * moment_one + (1.0 - beta_one) * gradient
    fresh_two = beta_two * moment_two + (1.0 - beta_two) * gradient * gradient
    return (fresh_one, fresh_two)


def direction_of(fresh_one, fresh_two, master):
    return fresh_one / bias_one / (jnp.sqrt(fresh_two / bias_two) + adam_eps) + decay_rate * master


def _bit(value, k):
    return (value >> k) & 1


def _exchange(x, pairs):
    return lax.ppermute(x, ("rep", "shard"), pairs)


def _swap(block, vector, pairs):
    other, vec_other = _exchange((block, vector), pairs)
    return lax.optimization_barrier((other, vec_other))


def _reduce_gradient(cotangents, activations, grad_scale, vector, rep_count, shard_count, rows):
    total = rep_count * shard_count
    chips = shard_count // 2
    tok_count, width = activations.shape
    rep_bits = rep_count.bit_length() - 1
    chip_bits = chips.bit_length() - 1
    slice_rows = rows // rep_count
    rep_idx = lax.axis_index("rep")
    shard_idx = lax.axis_index("shard")
    core = shard_idx % 2
    chip = shard_idx // 2
    contract = (((0,), (0,)), ((), ()))

    def core_of(i):
        return (i % shard_count) % 2

    grad_term = (
        lax.dot_general(cotangents, activations, contract, preferred_element_type=jnp.float32)
        * grad_scale
    )

    split = grad_term.reshape(chips, 2, rows, width)
    keep = lax.dynamic_index_in_dim(split, core, axis=1, keepdims=False)
    send = lax.dynamic_index_in_dim(split, 1 - core, axis=1, keepdims=False)
    other, vec_other = _swap(send, vector, [(i, i ^ 1) for i in range(total)])
    held = keep + other
    vector = vector + vec_other

    orders = (list(range(rep_bits)), list(reversed(range(rep_bits))))
    held = held.reshape(chips, rep_count, slice_rows, width)
    picks = []
    for j in range(rep_bits):
        pick = jnp.where(core == 0, _bit(rep_idx, orders[0][j]), _bit(rep_idx, orders[1][j]))
        picks.append(pick)
        pairs = [(i, i ^ ((1 << orders[core_of(i)][j]) * shard_count)) for i in range(total)]
        halves = held.reshape(chips, 2, -1, slice_rows, width)
        keep = lax.dynamic_index_in_dim(halves, pick, axis=1, keepdims=False)
        send = lax.dynamic_index_in_dim(halves, 1 - pick, axis=1, keepdims=False)
        other, vec_other = _swap(send, vector, pairs)
        held = keep + other
        vector = vector + vec_other
    held = held.reshape(chips, slice_rows, width)

    for j in range(chip_bits):
        pick = _bit(chip, j)
        pairs = [(i, i ^ ((1 << j) * 2)) for i in range(total)]
        halves = held.reshape(chips >> (j + 1), 2, slice_rows, width)
        keep = lax.dynamic_index_in_dim(halves, pick, axis=1, keepdims=False)
        send = lax.dynamic_index_in_dim(halves, 1 - pick, axis=1, keepdims=False)
        other, vec_other = _swap(send, vector, pairs)
        held = keep + other
        vector = vector + vec_other
    held = held.reshape(slice_rows, width)
    slice_idx = 0
    for j in range(rep_bits):
        slice_idx = slice_idx * 2 + picks[j]
    own_slice = held

    for j in reversed(range(rep_bits)):
        pick = picks[j]
        pairs = [(i, i ^ ((1 << orders[core_of(i)][j]) * shard_count)) for i in range(total)]
        other = _exchange(held, pairs)
        low = jnp.where(pick == 0, held, other)
        high = jnp.where(pick == 0, other, held)
        held = jnp.concatenate([low[None], high[None]], axis=0).reshape(-1, width)
    return held, vector, own_slice, slice_idx * slice_rows


def _sum_everywhere(values, shard_count, rep_count):
    total = rep_count * shard_count

    def gathered_sum(part, count, stride, own):
        got = [part]
        for d in range(1, count):
            pairs = []
            for i in range(total):
                group, pos = divmod(i // stride, count)
                rest = i % stride
                pairs.append((i, (group * count + (pos + d) % count) * stride + rest))
            got.append(_exchange(part, pairs))
        stacked = jnp.roll(jnp.stack(got[::-1]), own + 1, axis=0)
        return jnp.sum(stacked, axis=0)

    values = gathered_sum(values, shard_count, 1, lax.axis_index("shard"))
    return gathered_sum(values, rep_count, shard_count, lax.axis_index("rep"))


def _gather_over_shard(values, shard_count, rep_count):
    total = rep_count * shard_count
    shard_idx = lax.axis_index("shard")
    held = values[None]
    for j in range(shard_count.bit_length() - 1):
        other = _exchange(held, [(i, i ^ (1 << j)) for i in range(total)])
        mine_low = _bit(shard_idx, j) == 0
        low = jnp.where(mine_low, held, other)
        high = jnp.where(mine_low, other, held)
        held = jnp.concatenate([low, high], axis=0)
    return held


def per_device(
    activations,
    cotangents,
    grad_vectors,
    master_matrix,
    first_matrix,
    second_matrix,
    master_vector,
    first_vector,
    second_vector,
):
    rep_count = lax.axis_size("rep")
    shard_count = lax.axis_size("shard")
    tok_count, model_width = activations.shape
    rows = master_matrix.shape[0]
    grad_scale = 1.0 / math.sqrt(tok_count * rep_count * shard_count)
    shard_idx = lax.axis_index("shard")
    vector_term = grad_vectors[0].astype(jnp.float32) * grad_scale
    weight_sq = jnp.sum(master_matrix * master_matrix)
    vector_sq = jnp.sum(master_vector * master_vector, axis=1)
    grad_rows, vector_sum, grad_slice, slice_start = _reduce_gradient(
        cotangents, activations, grad_scale, vector_term, rep_count, shard_count, rows
    )
    grad_vecs = lax.dynamic_slice_in_dim(vector_sum, shard_idx * rows, rows, axis=1)
    first_vecs, second_vecs = moments(grad_vecs, first_vector, second_vector)
    update_vec = direction_of(first_vecs, second_vecs, master_vector)
    upvector_sq = jnp.sum(update_vec * update_vec, axis=1)
    slice_of = lambda a: lax.dynamic_slice_in_dim(a, slice_start, grad_slice.shape[0], axis=0)
    first_slice, second_slice = moments(grad_slice, slice_of(first_matrix), slice_of(second_matrix))
    update_slice = direction_of(first_slice, second_slice, slice_of(master_matrix))
    update_sq = jnp.sum(update_slice * update_slice)
    first_rep = lax.axis_index("rep") == 0
    replicated = jnp.concatenate([weight_sq[None], vector_sq, upvector_sq])
    replicated = jnp.where(first_rep, replicated, jnp.zeros_like(replicated))
    sums = _sum_everywhere(
        jnp.concatenate([replicated, update_sq[None]]), shard_count, rep_count
    )
    weight_tot, vector_tot, upvector_tot, update_tot = sums[0], sums[1:3], sums[3:5], sums[5]
    first_rows, second_rows = moments(grad_rows, first_matrix, second_matrix)
    update_matrix = direction_of(first_rows, second_rows, master_matrix)
    trust_matrix = jnp.sqrt(weight_tot) / jnp.sqrt(update_tot + norm_eps)
    trust_vec = (jnp.sqrt(vector_tot) / jnp.sqrt(upvector_tot + norm_eps))[:, None]
    stepped = master_matrix - learn_rate * trust_matrix * update_matrix
    master_rows = stepped / jnp.sqrt(jnp.mean(stepped * stepped, axis=1, keepdims=True) + norm_eps)
    master_vecs = master_vector - learn_rate * trust_vec * update_vec
    gathered_matrix = lax.all_gather(
        master_rows.astype(jnp.bfloat16), "shard", axis=0, tiled=True
    )
    gathered_vectors = _gather_over_shard(master_vecs.astype(jnp.bfloat16), shard_count, rep_count)
    gathered_vectors = gathered_vectors.transpose(1, 0, 2).reshape(2, shard_count * rows)
    return (
        gathered_matrix,
        gathered_vectors,
        master_rows,
        first_rows,
        second_rows,
        master_vecs,
        first_vecs,
        second_vecs,
    )


def solution(mesh):
    placed = (
        P(("rep", "shard"), None),
        P(("rep", "shard"), None),
        P(("rep", "shard"), None, None),
        P("shard", None),
        P("shard", None),
        P("shard", None),
        P(None, "shard"),
        P(None, "shard"),
        P(None, "shard"),
    )
    return jax.shard_map(
        per_device,
        mesh=mesh,
        in_specs=placed,
        out_specs=(
            P(),
            P(),
            P("shard", None),
            P("shard", None),
            P("shard", None),
            P(None, "shard"),
            P(None, "shard"),
            P(None, "shard"),
        ),
        check_vma=False,
    )
```

```python
import math

import jax
import jax.numpy as jnp
from jax import lax
from jax.sharding import PartitionSpec as P

beta_one = 0.9
beta_two = 0.95
adam_eps = 1e-08
decay_rate = 0.1
learn_rate = 0.2
bias_one = 0.9999734386011124
bias_two = 0.994079470779666
norm_eps = 1e-06


def moments(gradient, moment_one, moment_two):
    fresh_one = beta_one * moment_one + (1.0 - beta_one) * gradient
    fresh_two = beta_two * moment_two + (1.0 - beta_two) * gradient * gradient
    return (fresh_one, fresh_two)


def direction_of(fresh_one, fresh_two, master):
    return fresh_one / bias_one / (jnp.sqrt(fresh_two / bias_two) + adam_eps) + decay_rate * master


def _bit(value, k):
    return (value >> k) & 1


def _exchange(x, pairs):
    return lax.ppermute(x, ("rep", "shard"), pairs)


def _swap(block, vector, pairs):
    other, vec_other = _exchange((block, vector), pairs)
    return lax.optimization_barrier((other, vec_other))


def _reduce_gradient(cotangents, activations, grad_scale, vector, rep_count, shard_count, rows):
    total = rep_count * shard_count
    chips = shard_count // 2
    tok_count, width = activations.shape
    rep_bits = rep_count.bit_length() - 1
    chip_bits = chips.bit_length() - 1
    slice_rows = rows // rep_count
    rep_idx = lax.axis_index("rep")
    shard_idx = lax.axis_index("shard")
    core = shard_idx % 2
    chip = shard_idx // 2
    contract = (((0,), (0,)), ((), ()))

    def core_of(i):
        return (i % shard_count) % 2

    grad_term = (
        lax.dot_general(cotangents, activations, contract, preferred_element_type=jnp.float32)
        * grad_scale
    )

    split = grad_term.reshape(chips, 2, rows, width)
    keep = lax.dynamic_index_in_dim(split, core, axis=1, keepdims=False)
    send = lax.dynamic_index_in_dim(split, 1 - core, axis=1, keepdims=False)
    other, vec_other = _swap(send, vector, [(i, i ^ 1) for i in range(total)])
    held = keep + other
    vector = vector + vec_other

    orders = (list(range(rep_bits)), list(reversed(range(rep_bits))))
    held = held.reshape(chips, rep_count, slice_rows, width)
    picks = []
    for j in range(rep_bits):
        pick = jnp.where(core == 0, _bit(rep_idx, orders[0][j]), _bit(rep_idx, orders[1][j]))
        picks.append(pick)
        pairs = [(i, i ^ ((1 << orders[core_of(i)][j]) * shard_count)) for i in range(total)]
        halves = held.reshape(chips, 2, -1, slice_rows, width)
        keep = lax.dynamic_index_in_dim(halves, pick, axis=1, keepdims=False)
        send = lax.dynamic_index_in_dim(halves, 1 - pick, axis=1, keepdims=False)
        other, vec_other = _swap(send, vector, pairs)
        held = keep + other
        vector = vector + vec_other
    held = held.reshape(chips, slice_rows, width)

    for j in range(chip_bits):
        pick = _bit(chip, j)
        pairs = [(i, i ^ ((1 << j) * 2)) for i in range(total)]
        halves = held.reshape(chips >> (j + 1), 2, slice_rows, width)
        keep = lax.dynamic_index_in_dim(halves, pick, axis=1, keepdims=False)
        send = lax.dynamic_index_in_dim(halves, 1 - pick, axis=1, keepdims=False)
        other, vec_other = _swap(send, vector, pairs)
        held = keep + other
        vector = vector + vec_other
    held = held.reshape(slice_rows, width)

    for j in reversed(range(rep_bits)):
        pick = picks[j]
        pairs = [(i, i ^ ((1 << orders[core_of(i)][j]) * shard_count)) for i in range(total)]
        other = _exchange(held, pairs)
        low = jnp.where(pick == 0, held, other)
        high = jnp.where(pick == 0, other, held)
        held = jnp.concatenate([low[None], high[None]], axis=0).reshape(-1, width)
    return held, vector


def _sum_over_shard(values, shard_count, rep_count):
    total = rep_count * shard_count
    for j in range(shard_count.bit_length() - 1):
        values = values + _exchange(values, [(i, i ^ (1 << j)) for i in range(total)])
    return values


def _gather_over_shard(values, shard_count, rep_count):
    total = rep_count * shard_count
    shard_idx = lax.axis_index("shard")
    held = values[None]
    for j in range(shard_count.bit_length() - 1):
        other = _exchange(held, [(i, i ^ (1 << j)) for i in range(total)])
        mine_low = _bit(shard_idx, j) == 0
        low = jnp.where(mine_low, held, other)
        high = jnp.where(mine_low, other, held)
        held = jnp.concatenate([low, high], axis=0)
    return held


def per_device(
    activations,
    cotangents,
    grad_vectors,
    master_matrix,
    first_matrix,
    second_matrix,
    master_vector,
    first_vector,
    second_vector,
):
    rep_count = lax.axis_size("rep")
    shard_count = lax.axis_size("shard")
    tok_count, model_width = activations.shape
    rows = master_matrix.shape[0]
    grad_scale = 1.0 / math.sqrt(tok_count * rep_count * shard_count)
    shard_idx = lax.axis_index("shard")
    vector_term = grad_vectors[0].astype(jnp.float32) * grad_scale
    weight_sq = jnp.sum(master_matrix * master_matrix)
    vector_sq = jnp.sum(master_vector * master_vector, axis=1)
    grad_rows, vector_sum = _reduce_gradient(
        cotangents, activations, grad_scale, vector_term, rep_count, shard_count, rows
    )
    grad_vecs = lax.dynamic_slice_in_dim(vector_sum, shard_idx * rows, rows, axis=1)
    first_rows, second_rows = moments(grad_rows, first_matrix, second_matrix)
    first_vecs, second_vecs = moments(grad_vecs, first_vector, second_vector)
    update_matrix = direction_of(first_rows, second_rows, master_matrix)
    update_vec = direction_of(first_vecs, second_vecs, master_vector)
    update_sq = jnp.sum(update_matrix * update_matrix)
    upvector_sq = jnp.sum(update_vec * update_vec, axis=1)
    sums = jnp.concatenate(
        [weight_sq[None], vector_sq, update_sq[None], upvector_sq]
    )
    sums = _sum_over_shard(sums, shard_count, rep_count)
    weight_tot, vector_tot, update_tot, upvector_tot = sums[0], sums[1:3], sums[3], sums[4:6]
    trust_matrix = jnp.sqrt(weight_tot) / jnp.sqrt(update_tot + norm_eps)
    trust_vec = (jnp.sqrt(vector_tot) / jnp.sqrt(upvector_tot + norm_eps))[:, None]
    stepped = master_matrix - learn_rate * trust_matrix * update_matrix
    master_rows = stepped / jnp.sqrt(jnp.mean(stepped * stepped, axis=1, keepdims=True) + norm_eps)
    master_vecs = master_vector - learn_rate * trust_vec * update_vec
    quarter = rows // rep_count
    own_quarter = lax.dynamic_slice_in_dim(
        master_rows.astype(jnp.bfloat16), lax.axis_index("rep") * quarter, quarter, axis=0
    )
    gathered_matrix = lax.all_gather(own_quarter, ("shard", "rep"), axis=0, tiled=True)
    gathered_vectors = _gather_over_shard(master_vecs.astype(jnp.bfloat16), shard_count, rep_count)
    gathered_vectors = gathered_vectors.transpose(1, 0, 2).reshape(2, shard_count * rows)
    return (
        gathered_matrix,
        gathered_vectors,
        master_rows,
        first_rows,
        second_rows,
        master_vecs,
        first_vecs,
        second_vecs,
    )


def solution(mesh):
    placed = (
        P(("rep", "shard"), None),
        P(("rep", "shard"), None),
        P(("rep", "shard"), None, None),
        P("shard", None),
        P("shard", None),
        P("shard", None),
        P(None, "shard"),
        P(None, "shard"),
        P(None, "shard"),
    )
    return jax.shard_map(
        per_device,
        mesh=mesh,
        in_specs=placed,
        out_specs=(
            P(),
            P(),
            P("shard", None),
            P("shard", None),
            P("shard", None),
            P(None, "shard"),
            P(None, "shard"),
            P(None, "shard"),
        ),
        check_vma=False,
    )
```

```python
import math

import jax
import jax.numpy as jnp
from jax import lax
from jax.sharding import PartitionSpec as P

beta_one = 0.9
beta_two = 0.95
adam_eps = 1e-08
decay_rate = 0.1
learn_rate = 0.2
bias_one = 0.9999734386011124
bias_two = 0.994079470779666
norm_eps = 1e-06


def moments(gradient, moment_one, moment_two):
    fresh_one = beta_one * moment_one + (1.0 - beta_one) * gradient
    fresh_two = beta_two * moment_two + (1.0 - beta_two) * gradient * gradient
    return (fresh_one, fresh_two)


def direction_of(fresh_one, fresh_two, master):
    return fresh_one / bias_one / (jnp.sqrt(fresh_two / bias_two) + adam_eps) + decay_rate * master


def _bit(value, k):
    return (value >> k) & 1


def _exchange(x, pairs):
    return lax.ppermute(x, ("rep", "shard"), pairs)


def _swap(block, vector, pairs):
    other, vec_other = _exchange((block, vector), pairs)
    return lax.optimization_barrier((other, vec_other))


def _reduce_gradient(cotangents, activations, grad_scale, vector, rep_count, shard_count, rows):
    total = rep_count * shard_count
    chips = shard_count // 2
    tok_count, width = activations.shape
    rep_bits = rep_count.bit_length() - 1
    chip_bits = chips.bit_length() - 1
    slice_rows = rows // rep_count
    rep_idx = lax.axis_index("rep")
    shard_idx = lax.axis_index("shard")
    core = shard_idx % 2
    chip = shard_idx // 2
    contract = (((0,), (0,)), ((), ()))

    def core_of(i):
        return (i % shard_count) % 2

    grad_term = (
        lax.dot_general(cotangents, activations, contract, preferred_element_type=jnp.float32)
        * grad_scale
    )

    split = grad_term.reshape(chips, 2, rows, width)
    keep = lax.dynamic_index_in_dim(split, core, axis=1, keepdims=False)
    send = lax.dynamic_index_in_dim(split, 1 - core, axis=1, keepdims=False)
    other, vec_other = _swap(send, vector, [(i, i ^ 1) for i in range(total)])
    held = keep + other
    vector = vector + vec_other

    orders = (list(range(rep_bits)), list(reversed(range(rep_bits))))
    picks = [
        jnp.where(core == 0, _bit(rep_idx, orders[0][j]), _bit(rep_idx, orders[1][j]))
        for j in range(rep_bits)
    ]
    rep_pairs = [
        [(i, i ^ ((1 << orders[core_of(i)][j]) * shard_count)) for i in range(total)]
        for j in range(rep_bits)
    ]

    def halving(shape, pick, pairs):
        def step(held):
            halves = held.reshape(shape)
            keep = lax.dynamic_index_in_dim(halves, pick, axis=1, keepdims=False)
            send = lax.dynamic_index_in_dim(halves, 1 - pick, axis=1, keepdims=False)
            return send, pairs, lambda got: keep + got
        return step

    def doubling(pick, pairs, cols):
        def step(held):
            held = held.reshape(-1, cols)
            def combine(got):
                low = jnp.where(pick == 0, held, got)
                high = jnp.where(pick == 0, got, held)
                return jnp.concatenate([low[None], high[None]], axis=0).reshape(-1, cols)
            return held, pairs, combine
        return step

    def steps_for(cols):
        steps = []
        for j in range(rep_bits):
            steps.append(halving((chips, 2, -1, slice_rows, cols), picks[j], rep_pairs[j]))
        for j in range(chip_bits):
            pairs = [(i, i ^ ((1 << j) * 2)) for i in range(total)]
            steps.append(halving((chips >> (j + 1), 2, slice_rows, cols), _bit(chip, j), pairs))
        for j in reversed(range(rep_bits)):
            steps.append(doubling(picks[j], rep_pairs[j], cols))
        return steps

    chunks = 2 if width % 256 == 0 else 1
    cols = width // chunks
    states = [held[:, :, c * cols : (c + 1) * cols] for c in range(chunks)]
    plans = [steps_for(cols) for _ in range(chunks)]
    vector_steps = rep_bits + chip_bits
    count = len(plans[0])
    for t in range(count + chunks - 1):
        active = [c for c in range(chunks) if 0 <= t - c < count]
        sends, combines = [], []
        for c in active:
            send, pairs, combine = plans[c][t - c](states[c])
            sends.append(_exchange(send, pairs))
            combines.append(combine)
        if t < vector_steps:
            _, pairs, _ = plans[0][t](states[0])
            sends.append(_exchange(vector, pairs))
        got, held_states = lax.optimization_barrier((tuple(sends), tuple(states)))
        states = list(held_states)
        for c, combine, arrived in zip(active, combines, got):
            states[c] = combine(arrived)
        if t < vector_steps:
            vector = vector + got[-1]
    held = jnp.concatenate([s.reshape(rows, cols) for s in states], axis=1)
    return held, vector


def _sum_over_shard(values, shard_count, rep_count):
    total = rep_count * shard_count
    for j in range(shard_count.bit_length() - 1):
        values = values + _exchange(values, [(i, i ^ (1 << j)) for i in range(total)])
    return values


def _gather_over_shard(values, shard_count, rep_count):
    total = rep_count * shard_count
    shard_idx = lax.axis_index("shard")
    held = values[None]
    for j in range(shard_count.bit_length() - 1):
        other = _exchange(held, [(i, i ^ (1 << j)) for i in range(total)])
        mine_low = _bit(shard_idx, j) == 0
        low = jnp.where(mine_low, held, other)
        high = jnp.where(mine_low, other, held)
        held = jnp.concatenate([low, high], axis=0)
    return held


def per_device(
    activations,
    cotangents,
    grad_vectors,
    master_matrix,
    first_matrix,
    second_matrix,
    master_vector,
    first_vector,
    second_vector,
):
    rep_count = lax.axis_size("rep")
    shard_count = lax.axis_size("shard")
    tok_count, model_width = activations.shape
    rows = master_matrix.shape[0]
    grad_scale = 1.0 / math.sqrt(tok_count * rep_count * shard_count)
    shard_idx = lax.axis_index("shard")
    vector_term = grad_vectors[0].astype(jnp.float32) * grad_scale
    weight_sq = jnp.sum(master_matrix * master_matrix)
    vector_sq = jnp.sum(master_vector * master_vector, axis=1)
    grad_rows, vector_sum = _reduce_gradient(
        cotangents, activations, grad_scale, vector_term, rep_count, shard_count, rows
    )
    grad_vecs = lax.dynamic_slice_in_dim(vector_sum, shard_idx * rows, rows, axis=1)
    first_rows, second_rows = moments(grad_rows, first_matrix, second_matrix)
    first_vecs, second_vecs = moments(grad_vecs, first_vector, second_vector)
    update_matrix = direction_of(first_rows, second_rows, master_matrix)
    update_vec = direction_of(first_vecs, second_vecs, master_vector)
    update_sq = jnp.sum(update_matrix * update_matrix)
    upvector_sq = jnp.sum(update_vec * update_vec, axis=1)
    sums = jnp.concatenate(
        [weight_sq[None], vector_sq, update_sq[None], upvector_sq]
    )
    sums = _sum_over_shard(sums, shard_count, rep_count)
    weight_tot, vector_tot, update_tot, upvector_tot = sums[0], sums[1:3], sums[3], sums[4:6]
    trust_matrix = jnp.sqrt(weight_tot) / jnp.sqrt(update_tot + norm_eps)
    trust_vec = (jnp.sqrt(vector_tot) / jnp.sqrt(upvector_tot + norm_eps))[:, None]
    stepped = master_matrix - learn_rate * trust_matrix * update_matrix
    master_rows = stepped / jnp.sqrt(jnp.mean(stepped * stepped, axis=1, keepdims=True) + norm_eps)
    master_vecs = master_vector - learn_rate * trust_vec * update_vec
    gathered_matrix = lax.all_gather(
        master_rows.astype(jnp.bfloat16), "shard", axis=0, tiled=True
    )
    gathered_vectors = _gather_over_shard(master_vecs.astype(jnp.bfloat16), shard_count, rep_count)
    gathered_vectors = gathered_vectors.transpose(1, 0, 2).reshape(2, shard_count * rows)
    return (
        gathered_matrix,
        gathered_vectors,
        master_rows,
        first_rows,
        second_rows,
        master_vecs,
        first_vecs,
        second_vecs,
    )


def solution(mesh):
    placed = (
        P(("rep", "shard"), None),
        P(("rep", "shard"), None),
        P(("rep", "shard"), None, None),
        P("shard", None),
        P("shard", None),
        P("shard", None),
        P(None, "shard"),
        P(None, "shard"),
        P(None, "shard"),
    )
    return jax.shard_map(
        per_device,
        mesh=mesh,
        in_specs=placed,
        out_specs=(
            P(),
            P(),
            P("shard", None),
            P("shard", None),
            P("shard", None),
            P(None, "shard"),
            P(None, "shard"),
            P(None, "shard"),
        ),
        check_vma=False,
    )
```

```python
import math

import jax
import jax.numpy as jnp
from jax import lax
from jax.sharding import PartitionSpec as P

beta_one = 0.9
beta_two = 0.95
adam_eps = 1e-08
decay_rate = 0.1
learn_rate = 0.2
bias_one = 0.9999734386011124
bias_two = 0.994079470779666
norm_eps = 1e-06


def moments(gradient, moment_one, moment_two):
    fresh_one = beta_one * moment_one + (1.0 - beta_one) * gradient
    fresh_two = beta_two * moment_two + (1.0 - beta_two) * gradient * gradient
    return (fresh_one, fresh_two)


def direction_of(fresh_one, fresh_two, master):
    return fresh_one / bias_one / (jnp.sqrt(fresh_two / bias_two) + adam_eps) + decay_rate * master


def _bit(value, k):
    return (value >> k) & 1


def _exchange(x, pairs):
    return lax.ppermute(x, ("rep", "shard"), pairs)


def _swap(block, vector, pairs):
    other, vec_other = _exchange((block, vector), pairs)
    return lax.optimization_barrier((other, vec_other))


def _reduce_gradient(cotangents, activations, grad_scale, vector, rep_count, shard_count, rows):
    total = rep_count * shard_count
    chips = shard_count // 2
    tok_count, width = activations.shape
    rep_bits = rep_count.bit_length() - 1
    chip_bits = chips.bit_length() - 1
    slice_rows = rows // rep_count
    rep_idx = lax.axis_index("rep")
    shard_idx = lax.axis_index("shard")
    core = shard_idx % 2
    chip = shard_idx // 2
    contract = (((0,), (0,)), ((), ()))

    def core_of(i):
        return (i % shard_count) % 2

    parts = 2 if chips % 2 == 0 and width % 256 == 0 else 1
    part_rows = rows * shard_count // parts
    pieces = []
    for p in range(parts):
        product = lax.dot_general(
            cotangents[:, p * part_rows : (p + 1) * part_rows],
            activations,
            contract,
            preferred_element_type=jnp.float32,
        )
        split = (product * grad_scale).reshape(chips // parts, 2, rows, width)
        keep = lax.dynamic_index_in_dim(split, core, axis=1, keepdims=False)
        send = lax.dynamic_index_in_dim(split, 1 - core, axis=1, keepdims=False)
        pairs = [(i, i ^ 1) for i in range(total)]
        if p == 0:
            other, vec_other = _swap(send, vector, pairs)
            vector = vector + vec_other
        else:
            other = _exchange(send, pairs)
        pieces.append(keep + other)
    held = jnp.concatenate(pieces, axis=0)

    orders = (list(range(rep_bits)), list(reversed(range(rep_bits))))
    picks = [
        jnp.where(core == 0, _bit(rep_idx, orders[0][j]), _bit(rep_idx, orders[1][j]))
        for j in range(rep_bits)
    ]
    rep_pairs = [
        [(i, i ^ ((1 << orders[core_of(i)][j]) * shard_count)) for i in range(total)]
        for j in range(rep_bits)
    ]

    def halving(shape, pick, pairs):
        def step(held):
            halves = held.reshape(shape)
            keep = lax.dynamic_index_in_dim(halves, pick, axis=1, keepdims=False)
            send = lax.dynamic_index_in_dim(halves, 1 - pick, axis=1, keepdims=False)
            return send, pairs, lambda got: keep + got
        return step

    def doubling(pick, pairs, cols):
        def step(held):
            held = held.reshape(-1, cols)
            def combine(got):
                low = jnp.where(pick == 0, held, got)
                high = jnp.where(pick == 0, got, held)
                return jnp.concatenate([low[None], high[None]], axis=0).reshape(-1, cols)
            return held, pairs, combine
        return step

    def steps_for(cols):
        steps = []
        for j in range(rep_bits):
            steps.append(halving((chips, 2, -1, slice_rows, cols), picks[j], rep_pairs[j]))
        for j in range(chip_bits):
            pairs = [(i, i ^ ((1 << j) * 2)) for i in range(total)]
            steps.append(halving((chips >> (j + 1), 2, slice_rows, cols), _bit(chip, j), pairs))
        for j in reversed(range(rep_bits)):
            steps.append(doubling(picks[j], rep_pairs[j], cols))
        return steps

    chunks = 2 if width % 256 == 0 else 1
    cols = width // chunks
    states = [held[:, :, c * cols : (c + 1) * cols] for c in range(chunks)]
    plans = [steps_for(cols) for _ in range(chunks)]
    vector_steps = rep_bits + chip_bits
    count = len(plans[0])
    for t in range(count + chunks - 1):
        active = [c for c in range(chunks) if 0 <= t - c < count]
        sends, combines = [], []
        for c in active:
            send, pairs, combine = plans[c][t - c](states[c])
            sends.append(_exchange(send, pairs))
            combines.append(combine)
        if t < vector_steps:
            _, pairs, _ = plans[0][t](states[0])
            sends.append(_exchange(vector, pairs))
        got, held_states = lax.optimization_barrier((tuple(sends), tuple(states)))
        states = list(held_states)
        for c, combine, arrived in zip(active, combines, got):
            states[c] = combine(arrived)
        if t < vector_steps:
            vector = vector + got[-1]
    held = jnp.concatenate([s.reshape(rows, cols) for s in states], axis=1)
    return held, vector


def _sum_over_shard(values, shard_count, rep_count):
    total = rep_count * shard_count
    for j in range(shard_count.bit_length() - 1):
        values = values + _exchange(values, [(i, i ^ (1 << j)) for i in range(total)])
    return values


def _gather_over_shard(values, shard_count, rep_count):
    total = rep_count * shard_count
    shard_idx = lax.axis_index("shard")
    held = values[None]
    for j in range(shard_count.bit_length() - 1):
        other = _exchange(held, [(i, i ^ (1 << j)) for i in range(total)])
        mine_low = _bit(shard_idx, j) == 0
        low = jnp.where(mine_low, held, other)
        high = jnp.where(mine_low, other, held)
        held = jnp.concatenate([low, high], axis=0)
    return held


def per_device(
    activations,
    cotangents,
    grad_vectors,
    master_matrix,
    first_matrix,
    second_matrix,
    master_vector,
    first_vector,
    second_vector,
):
    rep_count = lax.axis_size("rep")
    shard_count = lax.axis_size("shard")
    tok_count, model_width = activations.shape
    rows = master_matrix.shape[0]
    grad_scale = 1.0 / math.sqrt(tok_count * rep_count * shard_count)
    shard_idx = lax.axis_index("shard")
    vector_term = grad_vectors[0].astype(jnp.float32) * grad_scale
    weight_sq = jnp.sum(master_matrix * master_matrix)
    vector_sq = jnp.sum(master_vector * master_vector, axis=1)
    grad_rows, vector_sum = _reduce_gradient(
        cotangents, activations, grad_scale, vector_term, rep_count, shard_count, rows
    )
    grad_vecs = lax.dynamic_slice_in_dim(vector_sum, shard_idx * rows, rows, axis=1)
    first_rows, second_rows = moments(grad_rows, first_matrix, second_matrix)
    first_vecs, second_vecs = moments(grad_vecs, first_vector, second_vector)
    update_matrix = direction_of(first_rows, second_rows, master_matrix)
    update_vec = direction_of(first_vecs, second_vecs, master_vector)
    update_sq = jnp.sum(update_matrix * update_matrix)
    upvector_sq = jnp.sum(update_vec * update_vec, axis=1)
    sums = jnp.concatenate(
        [weight_sq[None], vector_sq, update_sq[None], upvector_sq]
    )
    sums = _sum_over_shard(sums, shard_count, rep_count)
    weight_tot, vector_tot, update_tot, upvector_tot = sums[0], sums[1:3], sums[3], sums[4:6]
    trust_matrix = jnp.sqrt(weight_tot) / jnp.sqrt(update_tot + norm_eps)
    trust_vec = (jnp.sqrt(vector_tot) / jnp.sqrt(upvector_tot + norm_eps))[:, None]
    stepped = master_matrix - learn_rate * trust_matrix * update_matrix
    master_rows = stepped / jnp.sqrt(jnp.mean(stepped * stepped, axis=1, keepdims=True) + norm_eps)
    master_vecs = master_vector - learn_rate * trust_vec * update_vec
    gathered_matrix = lax.all_gather(
        master_rows.astype(jnp.bfloat16), "shard", axis=0, tiled=True
    )
    gathered_vectors = _gather_over_shard(master_vecs.astype(jnp.bfloat16), shard_count, rep_count)
    gathered_vectors = gathered_vectors.transpose(1, 0, 2).reshape(2, shard_count * rows)
    return (
        gathered_matrix,
        gathered_vectors,
        master_rows,
        first_rows,
        second_rows,
        master_vecs,
        first_vecs,
        second_vecs,
    )


def solution(mesh):
    placed = (
        P(("rep", "shard"), None),
        P(("rep", "shard"), None),
        P(("rep", "shard"), None, None),
        P("shard", None),
        P("shard", None),
        P("shard", None),
        P(None, "shard"),
        P(None, "shard"),
        P(None, "shard"),
    )
    return jax.shard_map(
        per_device,
        mesh=mesh,
        in_specs=placed,
        out_specs=(
            P(),
            P(),
            P("shard", None),
            P("shard", None),
            P("shard", None),
            P(None, "shard"),
            P(None, "shard"),
            P(None, "shard"),
        ),
        check_vma=False,
    )
```

```python
import math

import jax
import jax.numpy as jnp
from jax import lax
from jax.sharding import PartitionSpec as P

beta_one = 0.9
beta_two = 0.95
adam_eps = 1e-08
decay_rate = 0.1
learn_rate = 0.2
bias_one = 0.9999734386011124
bias_two = 0.994079470779666
norm_eps = 1e-06


def moments(gradient, moment_one, moment_two):
    fresh_one = beta_one * moment_one + (1.0 - beta_one) * gradient
    fresh_two = beta_two * moment_two + (1.0 - beta_two) * gradient * gradient
    return (fresh_one, fresh_two)


def direction_of(fresh_one, fresh_two, master):
    return fresh_one / bias_one / (jnp.sqrt(fresh_two / bias_two) + adam_eps) + decay_rate * master


def _bit(value, k):
    return (value >> k) & 1


def _exchange(x, pairs):
    return lax.ppermute(x, ("rep", "shard"), pairs)


def _swap(block, vector, pairs):
    other, vec_other = _exchange((block, vector), pairs)
    return lax.optimization_barrier((other, vec_other))


def _reduce_gradient(cotangents, activations, grad_scale, vector, rep_count, shard_count, rows):
    total = rep_count * shard_count
    chips = shard_count // 2
    tok_count, width = activations.shape
    rep_bits = rep_count.bit_length() - 1
    chip_bits = chips.bit_length() - 1
    slice_rows = rows // rep_count
    rep_idx = lax.axis_index("rep")
    shard_idx = lax.axis_index("shard")
    core = shard_idx % 2
    chip = shard_idx // 2
    contract = (((0,), (0,)), ((), ()))

    def core_of(i):
        return (i % shard_count) % 2

    parts = 2 if chips % 2 == 0 and width % 256 == 0 else 1
    part_rows = rows * shard_count // parts
    pieces = []
    for p in range(parts):
        product = lax.dot_general(
            cotangents[:, p * part_rows : (p + 1) * part_rows],
            activations,
            contract,
            preferred_element_type=jnp.float32,
        )
        split = (product * grad_scale).reshape(chips // parts, 2, rows, width)
        keep = lax.dynamic_index_in_dim(split, core, axis=1, keepdims=False)
        send = lax.dynamic_index_in_dim(split, 1 - core, axis=1, keepdims=False)
        pairs = [(i, i ^ 1) for i in range(total)]
        if p == 0:
            other, vec_other = _swap(send, vector, pairs)
            vector = vector + vec_other
        else:
            other = _exchange(send, pairs)
        pieces.append(keep + other)
    held = jnp.concatenate(pieces, axis=0)

    orders = (list(range(rep_bits)), list(reversed(range(rep_bits))))
    picks = [
        jnp.where(core == 0, _bit(rep_idx, orders[0][j]), _bit(rep_idx, orders[1][j]))
        for j in range(rep_bits)
    ]
    rep_pairs = [
        [(i, i ^ ((1 << orders[core_of(i)][j]) * shard_count)) for i in range(total)]
        for j in range(rep_bits)
    ]

    def halving(shape, pick, pairs):
        def step(held):
            halves = held.reshape(shape)
            keep = lax.dynamic_index_in_dim(halves, pick, axis=1, keepdims=False)
            send = lax.dynamic_index_in_dim(halves, 1 - pick, axis=1, keepdims=False)
            return send, pairs, lambda got: keep + got
        return step

    def doubling(pick, pairs, cols):
        def step(held):
            held = held.reshape(-1, cols)
            def combine(got):
                low = jnp.where(pick == 0, held, got)
                high = jnp.where(pick == 0, got, held)
                return jnp.concatenate([low[None], high[None]], axis=0).reshape(-1, cols)
            return held, pairs, combine
        return step

    def steps_for(cols):
        steps = []
        for j in range(rep_bits):
            steps.append(halving((chips, 2, -1, slice_rows, cols), picks[j], rep_pairs[j]))
        for j in range(chip_bits):
            pairs = [(i, i ^ ((1 << j) * 2)) for i in range(total)]
            steps.append(halving((chips >> (j + 1), 2, slice_rows, cols), _bit(chip, j), pairs))
        for j in reversed(range(rep_bits)):
            steps.append(doubling(picks[j], rep_pairs[j], cols))
        return steps

    chunks = 2 if width % 256 == 0 else 1
    cols = width // chunks
    states = [held[:, :, c * cols : (c + 1) * cols] for c in range(chunks)]
    plans = [steps_for(cols) for _ in range(chunks)]
    vector_steps = rep_bits + chip_bits
    count = len(plans[0])
    for t in range(count + chunks - 1):
        active = [c for c in range(chunks) if 0 <= t - c < count]
        sends, combines = [], []
        for c in active:
            send, pairs, combine = plans[c][t - c](states[c])
            sends.append(_exchange(send, pairs))
            combines.append(combine)
        if t < vector_steps:
            _, pairs, _ = plans[0][t](states[0])
            sends.append(_exchange(vector, pairs))
        got, held_states = lax.optimization_barrier((tuple(sends), tuple(states)))
        states = list(held_states)
        for c, combine, arrived in zip(active, combines, got):
            states[c] = combine(arrived)
        if t < vector_steps:
            vector = vector + got[-1]
    states = [s.reshape(rows, cols) for s in states]
    return jnp.concatenate(states, axis=1), vector, states


def _sum_over_shard(values, shard_count, rep_count):
    total = rep_count * shard_count
    for j in range(shard_count.bit_length() - 1):
        values = values + _exchange(values, [(i, i ^ (1 << j)) for i in range(total)])
    return values


def _gather_over_shard(values, shard_count, rep_count):
    total = rep_count * shard_count
    shard_idx = lax.axis_index("shard")
    held = values[None]
    for j in range(shard_count.bit_length() - 1):
        other = _exchange(held, [(i, i ^ (1 << j)) for i in range(total)])
        mine_low = _bit(shard_idx, j) == 0
        low = jnp.where(mine_low, held, other)
        high = jnp.where(mine_low, other, held)
        held = jnp.concatenate([low, high], axis=0)
    return held


def per_device(
    activations,
    cotangents,
    grad_vectors,
    master_matrix,
    first_matrix,
    second_matrix,
    master_vector,
    first_vector,
    second_vector,
):
    rep_count = lax.axis_size("rep")
    shard_count = lax.axis_size("shard")
    tok_count, model_width = activations.shape
    rows = master_matrix.shape[0]
    grad_scale = 1.0 / math.sqrt(tok_count * rep_count * shard_count)
    shard_idx = lax.axis_index("shard")
    vector_term = grad_vectors[0].astype(jnp.float32) * grad_scale
    weight_sq = jnp.sum(master_matrix * master_matrix)
    vector_sq = jnp.sum(master_vector * master_vector, axis=1)
    grad_rows, vector_sum, grad_chunks = _reduce_gradient(
        cotangents, activations, grad_scale, vector_term, rep_count, shard_count, rows
    )
    grad_vecs = lax.dynamic_slice_in_dim(vector_sum, shard_idx * rows, rows, axis=1)
    first_rows, second_rows = moments(grad_rows, first_matrix, second_matrix)
    first_vecs, second_vecs = moments(grad_vecs, first_vector, second_vector)
    update_matrix = direction_of(first_rows, second_rows, master_matrix)
    update_vec = direction_of(first_vecs, second_vecs, master_vector)
    update_sq = 0.0
    cols = model_width // len(grad_chunks)
    for c, chunk in enumerate(grad_chunks):
        part = lambda a: a[:, c * cols : (c + 1) * cols]
        first_part, second_part = moments(chunk, part(first_matrix), part(second_matrix))
        update_part = direction_of(first_part, second_part, part(master_matrix))
        update_sq = update_sq + jnp.sum(update_part * update_part)
    upvector_sq = jnp.sum(update_vec * update_vec, axis=1)
    sums = jnp.concatenate(
        [weight_sq[None], vector_sq, update_sq[None], upvector_sq]
    )
    sums = _sum_over_shard(sums, shard_count, rep_count)
    weight_tot, vector_tot, update_tot, upvector_tot = sums[0], sums[1:3], sums[3], sums[4:6]
    trust_matrix = jnp.sqrt(weight_tot) / jnp.sqrt(update_tot + norm_eps)
    trust_vec = (jnp.sqrt(vector_tot) / jnp.sqrt(upvector_tot + norm_eps))[:, None]
    stepped = master_matrix - learn_rate * trust_matrix * update_matrix
    master_rows = stepped / jnp.sqrt(jnp.mean(stepped * stepped, axis=1, keepdims=True) + norm_eps)
    master_vecs = master_vector - learn_rate * trust_vec * update_vec
    gathered_matrix = lax.all_gather(
        master_rows.astype(jnp.bfloat16), "shard", axis=0, tiled=True
    )
    gathered_vectors = _gather_over_shard(master_vecs.astype(jnp.bfloat16), shard_count, rep_count)
    gathered_vectors = gathered_vectors.transpose(1, 0, 2).reshape(2, shard_count * rows)
    return (
        gathered_matrix,
        gathered_vectors,
        master_rows,
        first_rows,
        second_rows,
        master_vecs,
        first_vecs,
        second_vecs,
    )


def solution(mesh):
    placed = (
        P(("rep", "shard"), None),
        P(("rep", "shard"), None),
        P(("rep", "shard"), None, None),
        P("shard", None),
        P("shard", None),
        P("shard", None),
        P(None, "shard"),
        P(None, "shard"),
        P(None, "shard"),
    )
    return jax.shard_map(
        per_device,
        mesh=mesh,
        in_specs=placed,
        out_specs=(
            P(),
            P(),
            P("shard", None),
            P("shard", None),
            P("shard", None),
            P(None, "shard"),
            P(None, "shard"),
            P(None, "shard"),
        ),
        check_vma=False,
    )
```

```python
import math

import jax
import jax.numpy as jnp
from jax import lax
from jax.sharding import PartitionSpec as P

beta_one = 0.9
beta_two = 0.95
adam_eps = 1e-08
decay_rate = 0.1
learn_rate = 0.2
bias_one = 0.9999734386011124
bias_two = 0.994079470779666
norm_eps = 1e-06


def moments(gradient, moment_one, moment_two):
    fresh_one = beta_one * moment_one + (1.0 - beta_one) * gradient
    fresh_two = beta_two * moment_two + (1.0 - beta_two) * gradient * gradient
    return (fresh_one, fresh_two)


def direction_of(fresh_one, fresh_two, master):
    return fresh_one / bias_one / (jnp.sqrt(fresh_two / bias_two) + adam_eps) + decay_rate * master


def _bit(value, k):
    return (value >> k) & 1


def _exchange(x, pairs):
    return lax.ppermute(x, ("rep", "shard"), pairs)


def _swap(block, vector, pairs):
    other, vec_other = _exchange((block, vector), pairs)
    return lax.optimization_barrier((other, vec_other))


def _reduce_gradient(cotangents, activations, grad_scale, vector, rep_count, shard_count, rows):
    total = rep_count * shard_count
    chips = shard_count // 2
    tok_count, width = activations.shape
    rep_bits = rep_count.bit_length() - 1
    chip_bits = chips.bit_length() - 1
    slice_rows = rows // rep_count
    rep_idx = lax.axis_index("rep")
    shard_idx = lax.axis_index("shard")
    core = shard_idx % 2
    chip = shard_idx // 2
    contract = (((0,), (0,)), ((), ()))

    def core_of(i):
        return (i % shard_count) % 2

    parts = 2 if chips % 2 == 0 and width % 256 == 0 else 1
    part_rows = rows * shard_count // parts
    pieces = []
    for p in range(parts):
        product = lax.dot_general(
            cotangents[:, p * part_rows : (p + 1) * part_rows],
            activations,
            contract,
            preferred_element_type=jnp.float32,
        )
        split = (product * grad_scale).reshape(chips // parts, 2, rows, width)
        keep = lax.dynamic_index_in_dim(split, core, axis=1, keepdims=False)
        send = lax.dynamic_index_in_dim(split, 1 - core, axis=1, keepdims=False)
        pairs = [(i, i ^ 1) for i in range(total)]
        if p == 0:
            other, vec_other = _swap(send, vector, pairs)
            vector = vector + vec_other
        else:
            other = _exchange(send, pairs)
        pieces.append((keep, other))
    held = tuple(jnp.concatenate([p[k] for p in pieces], axis=0) for k in range(2))

    orders = (list(range(rep_bits)), list(reversed(range(rep_bits))))
    picks = [
        jnp.where(core == 0, _bit(rep_idx, orders[0][j]), _bit(rep_idx, orders[1][j]))
        for j in range(rep_bits)
    ]
    rep_pairs = [
        [(i, i ^ ((1 << orders[core_of(i)][j]) * shard_count)) for i in range(total)]
        for j in range(rep_bits)
    ]

    def halving(shape, pick, pairs):
        def step(held):
            first, second = (h.reshape(shape) for h in held)
            part = lambda h, p: lax.dynamic_index_in_dim(h, p, axis=1, keepdims=False)
            send = part(first, 1 - pick) + part(second, 1 - pick)
            keep = part(first, pick) + part(second, pick)
            return send, pairs, lambda got: (keep, got)
        return step

    def doubling(pick, pairs, cols):
        def step(held):
            if isinstance(held, tuple):
                held = held[0] + held[1]
            held = held.reshape(-1, cols)
            def combine(got):
                low = jnp.where(pick == 0, held, got)
                high = jnp.where(pick == 0, got, held)
                return jnp.concatenate([low[None], high[None]], axis=0).reshape(-1, cols)
            return held, pairs, combine
        return step

    def steps_for(cols):
        steps = []
        for j in range(rep_bits):
            steps.append(halving((chips, 2, -1, slice_rows, cols), picks[j], rep_pairs[j]))
        for j in range(chip_bits):
            pairs = [(i, i ^ ((1 << j) * 2)) for i in range(total)]
            steps.append(halving((chips >> (j + 1), 2, slice_rows, cols), _bit(chip, j), pairs))
        for j in reversed(range(rep_bits)):
            steps.append(doubling(picks[j], rep_pairs[j], cols))
        return steps

    chunks = 2 if width % 256 == 0 else 1
    cols = width // chunks
    states = [tuple(h[:, :, c * cols : (c + 1) * cols] for h in held) for c in range(chunks)]
    plans = [steps_for(cols) for _ in range(chunks)]
    vector_steps = rep_bits + chip_bits
    count = len(plans[0])
    for t in range(count + chunks - 1):
        active = [c for c in range(chunks) if 0 <= t - c < count]
        sends, combines = [], []
        for c in active:
            send, pairs, combine = plans[c][t - c](states[c])
            sends.append(_exchange(send, pairs))
            combines.append(combine)
        if t < vector_steps:
            _, pairs, _ = plans[0][t](states[0])
            sends.append(_exchange(vector, pairs))
        got, held_states = lax.optimization_barrier((tuple(sends), tuple(states)))
        states = list(held_states)
        for c, combine, arrived in zip(active, combines, got):
            states[c] = combine(arrived)
        if t < vector_steps:
            vector = vector + got[-1]
    held = jnp.concatenate([s.reshape(rows, cols) for s in states], axis=1)
    return held, vector


def _sum_over_shard(values, shard_count, rep_count):
    total = rep_count * shard_count
    for j in range(shard_count.bit_length() - 1):
        values = values + _exchange(values, [(i, i ^ (1 << j)) for i in range(total)])
    return values


def _gather_over_shard(values, shard_count, rep_count):
    total = rep_count * shard_count
    shard_idx = lax.axis_index("shard")
    held = values[None]
    for j in range(shard_count.bit_length() - 1):
        other = _exchange(held, [(i, i ^ (1 << j)) for i in range(total)])
        mine_low = _bit(shard_idx, j) == 0
        low = jnp.where(mine_low, held, other)
        high = jnp.where(mine_low, other, held)
        held = jnp.concatenate([low, high], axis=0)
    return held


def per_device(
    activations,
    cotangents,
    grad_vectors,
    master_matrix,
    first_matrix,
    second_matrix,
    master_vector,
    first_vector,
    second_vector,
):
    rep_count = lax.axis_size("rep")
    shard_count = lax.axis_size("shard")
    tok_count, model_width = activations.shape
    rows = master_matrix.shape[0]
    grad_scale = 1.0 / math.sqrt(tok_count * rep_count * shard_count)
    shard_idx = lax.axis_index("shard")
    vector_term = grad_vectors[0].astype(jnp.float32) * grad_scale
    weight_sq = jnp.sum(master_matrix * master_matrix)
    vector_sq = jnp.sum(master_vector * master_vector, axis=1)
    grad_rows, vector_sum = _reduce_gradient(
        cotangents, activations, grad_scale, vector_term, rep_count, shard_count, rows
    )
    grad_vecs = lax.dynamic_slice_in_dim(vector_sum, shard_idx * rows, rows, axis=1)
    first_rows, second_rows = moments(grad_rows, first_matrix, second_matrix)
    first_vecs, second_vecs = moments(grad_vecs, first_vector, second_vector)
    update_matrix = direction_of(first_rows, second_rows, master_matrix)
    update_vec = direction_of(first_vecs, second_vecs, master_vector)
    update_sq = jnp.sum(update_matrix * update_matrix)
    upvector_sq = jnp.sum(update_vec * update_vec, axis=1)
    sums = jnp.concatenate(
        [weight_sq[None], vector_sq, update_sq[None], upvector_sq]
    )
    sums = _sum_over_shard(sums, shard_count, rep_count)
    weight_tot, vector_tot, update_tot, upvector_tot = sums[0], sums[1:3], sums[3], sums[4:6]
    trust_matrix = jnp.sqrt(weight_tot) / jnp.sqrt(update_tot + norm_eps)
    trust_vec = (jnp.sqrt(vector_tot) / jnp.sqrt(upvector_tot + norm_eps))[:, None]
    stepped = master_matrix - learn_rate * trust_matrix * update_matrix
    master_rows = stepped / jnp.sqrt(jnp.mean(stepped * stepped, axis=1, keepdims=True) + norm_eps)
    master_vecs = master_vector - learn_rate * trust_vec * update_vec
    gathered_matrix = lax.all_gather(
        master_rows.astype(jnp.bfloat16), "shard", axis=0, tiled=True
    )
    gathered_vectors = _gather_over_shard(master_vecs.astype(jnp.bfloat16), shard_count, rep_count)
    gathered_vectors = gathered_vectors.transpose(1, 0, 2).reshape(2, shard_count * rows)
    return (
        gathered_matrix,
        gathered_vectors,
        master_rows,
        first_rows,
        second_rows,
        master_vecs,
        first_vecs,
        second_vecs,
    )


def solution(mesh):
    placed = (
        P(("rep", "shard"), None),
        P(("rep", "shard"), None),
        P(("rep", "shard"), None, None),
        P("shard", None),
        P("shard", None),
        P("shard", None),
        P(None, "shard"),
        P(None, "shard"),
        P(None, "shard"),
    )
    return jax.shard_map(
        per_device,
        mesh=mesh,
        in_specs=placed,
        out_specs=(
            P(),
            P(),
            P("shard", None),
            P("shard", None),
            P("shard", None),
            P(None, "shard"),
            P(None, "shard"),
            P(None, "shard"),
        ),
        check_vma=False,
    )
```

```python
import math

import jax
import jax.numpy as jnp
from jax import lax
from jax.sharding import PartitionSpec as P

beta_one = 0.9
beta_two = 0.95
adam_eps = 1e-08
decay_rate = 0.1
learn_rate = 0.2
bias_one = 0.9999734386011124
bias_two = 0.994079470779666
norm_eps = 1e-06


def moments(gradient, moment_one, moment_two):
    fresh_one = beta_one * moment_one + (1.0 - beta_one) * gradient
    fresh_two = beta_two * moment_two + (1.0 - beta_two) * gradient * gradient
    return (fresh_one, fresh_two)


def direction_of(fresh_one, fresh_two, master):
    return fresh_one / bias_one / (jnp.sqrt(fresh_two / bias_two) + adam_eps) + decay_rate * master


def _bit(value, k):
    return (value >> k) & 1


def _exchange(x, pairs):
    return lax.ppermute(x, ("rep", "shard"), pairs)


def _swap(block, vector, pairs):
    other, vec_other = _exchange((block, vector), pairs)
    return lax.optimization_barrier((other, vec_other))


def _reduce_gradient(cotangents, activations, grad_scale, vector, rep_count, shard_count, rows):
    total = rep_count * shard_count
    chips = shard_count // 2
    tok_count, width = activations.shape
    rep_bits = rep_count.bit_length() - 1
    chip_bits = chips.bit_length() - 1
    slice_rows = rows // rep_count
    rep_idx = lax.axis_index("rep")
    shard_idx = lax.axis_index("shard")
    core = shard_idx % 2
    chip = shard_idx // 2
    contract = (((0,), (0,)), ((), ()))

    def core_of(i):
        return (i % shard_count) % 2

    parts = 2 if chips % 2 == 0 and width % 256 == 0 else 1
    part_rows = rows * shard_count // parts
    pieces = []
    for p in range(parts):
        product = lax.dot_general(
            cotangents[:, p * part_rows : (p + 1) * part_rows],
            activations,
            contract,
            preferred_element_type=jnp.float32,
        )
        split = (product * grad_scale).reshape(chips // parts, 2, rows, width)
        keep = lax.dynamic_index_in_dim(split, core, axis=1, keepdims=False)
        send = lax.dynamic_index_in_dim(split, 1 - core, axis=1, keepdims=False)
        pairs = [(i, i ^ 1) for i in range(total)]
        if p == parts - 1:
            other, vec_other = _swap(send, vector, pairs)
            vector = vector + vec_other
        else:
            other = _exchange(send, pairs)
        pieces.append(keep + other)
    held = jnp.concatenate(pieces, axis=0)

    orders = (list(range(rep_bits)), list(reversed(range(rep_bits))))
    picks = [
        jnp.where(core == 0, _bit(rep_idx, orders[0][j]), _bit(rep_idx, orders[1][j]))
        for j in range(rep_bits)
    ]
    rep_pairs = [
        [(i, i ^ ((1 << orders[core_of(i)][j]) * shard_count)) for i in range(total)]
        for j in range(rep_bits)
    ]

    def halving(shape, pick, pairs):
        def step(held):
            halves = held.reshape(shape)
            keep = lax.dynamic_index_in_dim(halves, pick, axis=1, keepdims=False)
            send = lax.dynamic_index_in_dim(halves, 1 - pick, axis=1, keepdims=False)
            return send, pairs, lambda got: keep + got
        return step

    def doubling(pick, pairs, cols):
        def step(held):
            held = held.reshape(-1, cols)
            def combine(got):
                low = jnp.where(pick == 0, held, got)
                high = jnp.where(pick == 0, got, held)
                return jnp.concatenate([low[None], high[None]], axis=0).reshape(-1, cols)
            return held, pairs, combine
        return step

    def steps_for(cols):
        steps = []
        for j in range(rep_bits):
            steps.append(halving((chips, 2, -1, slice_rows, cols), picks[j], rep_pairs[j]))
        for j in range(chip_bits):
            pairs = [(i, i ^ ((1 << j) * 2)) for i in range(total)]
            steps.append(halving((chips >> (j + 1), 2, slice_rows, cols), _bit(chip, j), pairs))
        for j in reversed(range(rep_bits)):
            steps.append(doubling(picks[j], rep_pairs[j], cols))
        return steps

    chunks = 2 if width % 256 == 0 else 1
    cols = width // chunks
    states = [held[:, :, c * cols : (c + 1) * cols] for c in range(chunks)]
    plans = [steps_for(cols) for _ in range(chunks)]
    vector_steps = rep_bits + chip_bits
    count = len(plans[0])
    for t in range(count + chunks - 1):
        active = [c for c in range(chunks) if 0 <= t - c < count]
        sends, combines = [], []
        for c in active:
            send, pairs, combine = plans[c][t - c](states[c])
            sends.append(_exchange(send, pairs))
            combines.append(combine)
        if t < vector_steps:
            _, pairs, _ = plans[0][t](states[0])
            sends.append(_exchange(vector, pairs))
        got, held_states = lax.optimization_barrier((tuple(sends), tuple(states)))
        states = list(held_states)
        for c, combine, arrived in zip(active, combines, got):
            states[c] = combine(arrived)
        if t < vector_steps:
            vector = vector + got[-1]
    held = jnp.concatenate([s.reshape(rows, cols) for s in states], axis=1)
    return held, vector


def _sum_over_shard(values, shard_count, rep_count):
    total = rep_count * shard_count
    for j in range(shard_count.bit_length() - 1):
        values = values + _exchange(values, [(i, i ^ (1 << j)) for i in range(total)])
    return values


def _gather_over_shard(values, shard_count, rep_count):
    total = rep_count * shard_count
    shard_idx = lax.axis_index("shard")
    held = values[None]
    for j in range(shard_count.bit_length() - 1):
        other = _exchange(held, [(i, i ^ (1 << j)) for i in range(total)])
        mine_low = _bit(shard_idx, j) == 0
        low = jnp.where(mine_low, held, other)
        high = jnp.where(mine_low, other, held)
        held = jnp.concatenate([low, high], axis=0)
    return held


def per_device(
    activations,
    cotangents,
    grad_vectors,
    master_matrix,
    first_matrix,
    second_matrix,
    master_vector,
    first_vector,
    second_vector,
):
    rep_count = lax.axis_size("rep")
    shard_count = lax.axis_size("shard")
    tok_count, model_width = activations.shape
    rows = master_matrix.shape[0]
    grad_scale = 1.0 / math.sqrt(tok_count * rep_count * shard_count)
    shard_idx = lax.axis_index("shard")
    vector_term = grad_vectors[0].astype(jnp.float32) * grad_scale
    weight_sq = jnp.sum(master_matrix * master_matrix)
    vector_sq = jnp.sum(master_vector * master_vector, axis=1)
    grad_rows, vector_sum = _reduce_gradient(
        cotangents, activations, grad_scale, vector_term, rep_count, shard_count, rows
    )
    grad_vecs = lax.dynamic_slice_in_dim(vector_sum, shard_idx * rows, rows, axis=1)
    first_rows, second_rows = moments(grad_rows, first_matrix, second_matrix)
    first_vecs, second_vecs = moments(grad_vecs, first_vector, second_vector)
    update_matrix = direction_of(first_rows, second_rows, master_matrix)
    update_vec = direction_of(first_vecs, second_vecs, master_vector)
    update_sq = jnp.sum(update_matrix * update_matrix)
    upvector_sq = jnp.sum(update_vec * update_vec, axis=1)
    sums = jnp.concatenate(
        [weight_sq[None], vector_sq, update_sq[None], upvector_sq]
    )
    sums = _sum_over_shard(sums, shard_count, rep_count)
    weight_tot, vector_tot, update_tot, upvector_tot = sums[0], sums[1:3], sums[3], sums[4:6]
    trust_matrix = jnp.sqrt(weight_tot) / jnp.sqrt(update_tot + norm_eps)
    trust_vec = (jnp.sqrt(vector_tot) / jnp.sqrt(upvector_tot + norm_eps))[:, None]
    stepped = master_matrix - learn_rate * trust_matrix * update_matrix
    master_rows = stepped / jnp.sqrt(jnp.mean(stepped * stepped, axis=1, keepdims=True) + norm_eps)
    master_vecs = master_vector - learn_rate * trust_vec * update_vec
    gathered_matrix = lax.all_gather(
        master_rows.astype(jnp.bfloat16), "shard", axis=0, tiled=True
    )
    gathered_vectors = _gather_over_shard(master_vecs.astype(jnp.bfloat16), shard_count, rep_count)
    gathered_vectors = gathered_vectors.transpose(1, 0, 2).reshape(2, shard_count * rows)
    return (
        gathered_matrix,
        gathered_vectors,
        master_rows,
        first_rows,
        second_rows,
        master_vecs,
        first_vecs,
        second_vecs,
    )


def solution(mesh):
    placed = (
        P(("rep", "shard"), None),
        P(("rep", "shard"), None),
        P(("rep", "shard"), None, None),
        P("shard", None),
        P("shard", None),
        P("shard", None),
        P(None, "shard"),
        P(None, "shard"),
        P(None, "shard"),
    )
    return jax.shard_map(
        per_device,
        mesh=mesh,
        in_specs=placed,
        out_specs=(
            P(),
            P(),
            P("shard", None),
            P("shard", None),
            P("shard", None),
            P(None, "shard"),
            P(None, "shard"),
            P(None, "shard"),
        ),
        check_vma=False,
    )
```
